256 devices in a mesh: tm: 32 (over x_lo, z, core), cell: 8 (over y, x_hi).
Axes of the slice: x: 4 (x_hi: 2, x_lo: 2; x = x_hi * 2 + x_lo), y: 4, z: 8, core: 2. Of those that a mesh axis runs over, the one named last changes fastest.
Arguments:
- velocity: bfloat16 [4096, 512, 96], P('cell', 'tm'), may hold values from -6 to 6
- cell_coords: int32 [4096, 3], P('cell'), may hold values from 0 to 15, as said below
- q_coords: int32 [512, 3], replicated, may hold values from 0 to 15
- eigvecs: float32 [512, 2, 96, 96], P(('tm', 'cell')), may hold values from -0.4375 to 0.4375
Outputs:
- power: float32 [512, 96, 512], P(('tm', 'cell'))
The draws below stay inside these ranges and needn't reach their ends.
Inputs may be any that keep to these rules, and one draw needn't show every extreme that they name: `cell_coords`: every row names a distinct lattice position, each coordinate in 0 to 15.
All inputs are finite; a program needn't handle non-finite values.
Results may differ from the reference program's by a relative error of at most 0.015.
Values may be sent and summed in bfloat16 or wider, within the bound.
No kernel may reach another device: no remote copies, remote signals or barrier semaphores. Data moves between devices by JAX's collectives and lax.ppermute only.
A program may use at most 64 MiB of HBM per device.

```python
import math
import jax
import jax.numpy as jnp
from jax import lax

CELL_DEV = 512
Q = 512
BR = 96
L = 16
NCELL = 4096
NF = 512
N_CELL = 8


def draw_cell_coords(key, part):
    cell_ids = jax.random.permutation(key, L * L * L)[:NCELL].astype(jnp.int32)
    return jnp.stack([cell_ids // (L * L), cell_ids // L % L, cell_ids % L], axis=1).astype(jnp.int32)


def set_ends(result, own_key, smallest, largest):
    dims = result.shape
    place = [jax.random.randint(jax.random.fold_in(own_key, axis), (), 0, dims[axis]) for axis in range(len(dims))]
    result = result.at[tuple(place)].set(smallest)
    longest = dims.index(max(dims))
    place[longest] = (place[longest] + 1) % dims[longest]
    return result.at[tuple(place)].set(largest)


def levels(own_key, dims, split, smallest, largest):
    factor_of = 1.0
    for axis_at, blocks in split:
        steps = jax.random.uniform(jax.random.fold_in(jax.random.fold_in(own_key, 6), axis_at), (blocks,), jnp.float32, smallest / len(split), largest / len(split))
        factor_of = factor_of * jnp.repeat(jnp.exp(steps), dims[axis_at] // blocks).reshape((-1,) + (1,) * (len(dims) - 1 - axis_at))
    return factor_of


def normal_values(key, extent, spread, bound, shards=(), kind=jnp.bfloat16):
    loudness = levels(key, extent, shards, -0.22, 0.18) if shards else 1.0
    result = jax.random.normal(key, extent, jnp.float32) * spread * loudness
    return jnp.minimum(jnp.maximum(result, -bound), bound).astype(kind)


def setup_inputs(seed: int = 0) -> dict:
    key_list = jax.random.split(jax.random.key(seed), 5)
    velocity = normal_values(key_list[0], (NCELL, NF, BR), 1.0, 6.0, ((0, 8), (1, 32)))
    cell_coords = draw_cell_coords(jax.random.fold_in(key_list[4], 71), 0)
    q_coords = set_ends(jax.random.randint(key_list[2], (Q, 3), 0, L), jax.random.fold_in(key_list[2], 1), 0, L - 1).astype(jnp.int32)
    eigvecs = normal_values(key_list[3], (Q, 2, BR, BR), (2 * BR) ** -0.5, 0.4375, ((0, 256),), jnp.float32)
    return {"velocity": velocity, "cell_coords": cell_coords, "q_coords": q_coords, "eigvecs": eigvecs}


def phase_rows(q_coords, cell_coords):
    products = (q_coords[:, None, 0] * cell_coords[None, :, 0] + q_coords[:, None, 1] * cell_coords[None, :, 1] + q_coords[:, None, 2] * cell_coords[None, :, 2]) % L
    angles = products.astype(jnp.float32) * (2.0 * math.pi / L)
    return jnp.stack([jnp.cos(angles), -jnp.sin(angles)], axis=1).astype(jnp.bfloat16)

def reference(velocity, cell_coords, q_coords, eigvecs):
    largest_value = lax.Precision.HIGHEST
    frames = velocity.shape[1]
    phase_table = phase_rows(q_coords, cell_coords)
    velocity_rows = velocity.reshape(N_CELL, CELL_DEV, frames * BR)
    table_blocks = phase_table.reshape(2 * Q, N_CELL, CELL_DEV).transpose(1, 0, 2)

    def add_block(running, block_pair):
        table_part, velocity_part = block_pair
        partial_sum = jnp.dot(table_part.astype(jnp.float32), velocity_part.astype(jnp.float32), precision=largest_value)
        rounded = lax.optimization_barrier(partial_sum.astype(jnp.bfloat16))
        return (running + rounded.astype(jnp.float32), None)
    running = lax.scan(add_block, jnp.zeros((2 * Q, frames * BR), jnp.float32), (table_blocks, velocity_rows))[0]
    cell_modes = running.reshape(Q, 2, frames, BR) * (1.0 / math.sqrt(N_CELL * CELL_DEV))
    normal_modes_real = cell_modes[:, 0]
    normal_modes_imaginary = cell_modes[:, 1]
    eigenvector_real = eigvecs[:, 0]
    eigenvector_imaginary = eigvecs[:, 1]
    amplitude_real = jnp.einsum('xcg,xga->xca', normal_modes_real, eigenvector_real, precision=largest_value) + jnp.einsum('xcg,xga->xca', normal_modes_imaginary, eigenvector_imaginary, precision=largest_value)
    amplitude_imaginary = jnp.einsum('xcg,xga->xca', normal_modes_imaginary, eigenvector_real, precision=largest_value) - jnp.einsum('xcg,xga->xca', normal_modes_real, eigenvector_imaginary, precision=largest_value)
    spectrum = jnp.fft.fft(amplitude_real + 1j * amplitude_imaginary, axis=1)
    power = (jnp.real(spectrum) ** 2 + jnp.imag(spectrum) ** 2) / frames
    return jnp.transpose(power, (0, 2, 1)).astype(jnp.float32)
```

```python
import math

import jax
import jax.numpy as jnp
from jax import lax
from jax.sharding import PartitionSpec as P

L = 16


def phase_rows(q_coords, cell_coords):
    products = (
        q_coords[:, None, 0] * cell_coords[None, :, 0]
        + q_coords[:, None, 1] * cell_coords[None, :, 1]
        + q_coords[:, None, 2] * cell_coords[None, :, 2]
    ) % L
    angles = products.astype(jnp.float32) * (2.0 * math.pi / L)
    return jnp.cos(angles).astype(jnp.bfloat16), (-jnp.sin(angles)).astype(jnp.bfloat16)


def twiddles(frames):
    inner = 16
    outer = frames // inner
    w = jnp.arange(frames, dtype=jnp.int32)
    a = jnp.arange(outer, dtype=jnp.int32)
    b = jnp.arange(inner, dtype=jnp.int32)
    coarse = (a[:, None] * w[None, :] % outer).astype(jnp.float32) * (2.0 * math.pi / outer)
    fine = (b[:, None] * w[None, :] % frames).astype(jnp.float32) * (2.0 * math.pi / frames)
    cos_c, sin_c = jnp.cos(coarse)[:, None, :], jnp.sin(coarse)[:, None, :]
    cos_f, sin_f = jnp.cos(fine)[None, :, :], jnp.sin(fine)[None, :, :]
    cosines = (cos_c * cos_f - sin_c * sin_f).reshape(frames, frames)
    sines = (sin_c * cos_f + cos_c * sin_f).reshape(frames, frames)
    return cosines, sines


def local(velocity, cell_coords, q_coords, eigvecs):
    n_tm = lax.axis_size("tm")
    n_cell = lax.axis_size("cell")
    cell_dev, frames_dev, branches = velocity.shape
    q_total = q_coords.shape[0]
    q_local = q_total // (n_tm * n_cell)
    frames = frames_dev * n_tm
    ordered_coords = (
        q_coords.reshape(n_tm, n_cell, q_local, 3).transpose(1, 0, 2, 3).reshape(q_total, 3)
    )
    cos_rows, sin_rows = phase_rows(ordered_coords, cell_coords)
    table = jnp.stack(
        [
            cos_rows.reshape(n_cell, n_tm * q_local, cell_dev),
            sin_rows.reshape(n_cell, n_tm * q_local, cell_dev),
        ],
        axis=1,
    ).reshape(2 * q_total, cell_dev)
    velocity_rows = velocity.reshape(cell_dev, frames_dev * branches)
    partial_term = jnp.dot(table, velocity_rows, preferred_element_type=jnp.float32)
    partial_term = partial_term.astype(jnp.bfloat16).reshape(
        n_cell, 2 * n_tm * q_local, frames_dev * branches
    )
    summed = lax.psum_scatter(partial_term, "cell", scatter_dimension=0, tiled=True)
    blocks = summed.reshape(2, n_tm, q_local, frames_dev, branches)
    collected = lax.all_to_all(blocks, "tm", split_axis=1, concat_axis=3, tiled=True)
    collected = collected.reshape(2, q_local, frames, branches).astype(jnp.float32)

    scale = 1.0 / math.sqrt(cell_dev * n_cell)
    e_real = eigvecs[:, 0] * scale
    e_imag = eigvecs[:, 1] * scale
    e_block = jnp.stack(
        [jnp.concatenate([e_real, -e_imag], axis=2), jnp.concatenate([e_imag, e_real], axis=2)],
        axis=1,
    )
    highest = lax.Precision.HIGHEST
    amplitude = jnp.einsum("rjtk,jrks->jts", collected, e_block, precision=highest)
    cosines, sines = twiddles(frames)
    basis = jnp.concatenate([cosines, sines], axis=1)
    projected = jnp.einsum("jts,tw->jsw", amplitude, basis, precision=highest)
    on_cos = projected[:, :, :frames]
    on_sin = projected[:, :, frames:]
    out_real = on_cos[:, :branches] + on_sin[:, branches:]
    out_imag = on_cos[:, branches:] - on_sin[:, :branches]
    return (out_real * out_real + out_imag * out_imag) / frames


def solution(mesh):
    in_specs = (P("cell", "tm", None), P("cell", None), P(), P(("tm", "cell"), None, None, None))
    out_specs = P(("tm", "cell"), None, None)
    return jax.shard_map(local, mesh=mesh, in_specs=in_specs, out_specs=out_specs, check_vma=False)
```

```python
import math

import jax
import jax.numpy as jnp
from jax import lax
from jax.sharding import PartitionSpec as P

L = 16


def phase_rows(q_coords, cell_coords):
    products = (
        q_coords[:, None, 0] * cell_coords[None, :, 0]
        + q_coords[:, None, 1] * cell_coords[None, :, 1]
        + q_coords[:, None, 2] * cell_coords[None, :, 2]
    ) % L
    angles = products.astype(jnp.float32) * (2.0 * math.pi / L)
    return jnp.cos(angles).astype(jnp.bfloat16), (-jnp.sin(angles)).astype(jnp.bfloat16)


def twiddles(frames):
    inner = 16
    outer = frames // inner
    w = jnp.arange(frames, dtype=jnp.int32)
    a = jnp.arange(outer, dtype=jnp.int32)
    b = jnp.arange(inner, dtype=jnp.int32)
    coarse = (a[:, None] * w[None, :] % outer).astype(jnp.float32) * (2.0 * math.pi / outer)
    fine = (b[:, None] * w[None, :] % frames).astype(jnp.float32) * (2.0 * math.pi / frames)
    cos_c, sin_c = jnp.cos(coarse)[:, None, :], jnp.sin(coarse)[:, None, :]
    cos_f, sin_f = jnp.cos(fine)[None, :, :], jnp.sin(fine)[None, :, :]
    cosines = (cos_c * cos_f - sin_c * sin_f).reshape(frames, frames)
    sines = (sin_c * cos_f + cos_c * sin_f).reshape(frames, frames)
    return cosines, sines


def local(velocity, cell_coords, q_coords, eigvecs):
    n_tm = lax.axis_size("tm")
    n_cell = lax.axis_size("cell")
    cell_dev, frames_dev, branches = velocity.shape
    q_total = q_coords.shape[0]
    q_local = q_total // (n_tm * n_cell)
    frames = frames_dev * n_tm
    ordered_coords = (
        q_coords.reshape(n_tm, n_cell, q_local, 3).transpose(1, 0, 2, 3).reshape(q_total, 3)
    )
    cos_rows, sin_rows = phase_rows(ordered_coords, cell_coords)
    table = jnp.stack(
        [
            cos_rows.reshape(n_cell, n_tm * q_local, cell_dev),
            sin_rows.reshape(n_cell, n_tm * q_local, cell_dev),
        ],
        axis=1,
    ).reshape(2 * q_total, cell_dev)
    velocity_rows = velocity.reshape(cell_dev, frames_dev * branches)
    partial_term = jnp.dot(table, velocity_rows, preferred_element_type=jnp.float32)
    partial_term = partial_term.astype(jnp.bfloat16).reshape(
        n_cell, 2 * n_tm * q_local, frames_dev * branches
    )
    gathered = lax.all_to_all(partial_term, "cell", split_axis=0, concat_axis=0, tiled=True)
    summed = jnp.sum(gathered.astype(jnp.float32), axis=0).astype(jnp.bfloat16)
    blocks = summed.reshape(2, n_tm, q_local, frames_dev, branches)
    collected = lax.all_to_all(blocks, "tm", split_axis=1, concat_axis=3, tiled=True)
    collected = collected.reshape(2, q_local, frames, branches).astype(jnp.float32)

    scale = 1.0 / math.sqrt(cell_dev * n_cell)
    e_real = eigvecs[:, 0] * scale
    e_imag = eigvecs[:, 1] * scale
    e_block = jnp.stack(
        [jnp.concatenate([e_real, -e_imag], axis=2), jnp.concatenate([e_imag, e_real], axis=2)],
        axis=1,
    )
    highest = lax.Precision.HIGHEST
    amplitude = jnp.einsum("rjtk,jrks->jts", collected, e_block, precision=highest)
    cosines, sines = twiddles(frames)
    basis = jnp.concatenate([cosines, sines], axis=1)
    projected = jnp.einsum("jts,tw->jsw", amplitude, basis, precision=highest)
    on_cos = projected[:, :, :frames]
    on_sin = projected[:, :, frames:]
    out_real = on_cos[:, :branches] + on_sin[:, branches:]
    out_imag = on_cos[:, branches:] - on_sin[:, :branches]
    return (out_real * out_real + out_imag * out_imag) / frames


def solution(mesh):
    in_specs = (P("cell", "tm", None), P("cell", None), P(), P(("tm", "cell"), None, None, None))
    out_specs = P(("tm", "cell"), None, None)
    return jax.shard_map(local, mesh=mesh, in_specs=in_specs, out_specs=out_specs, check_vma=False)
```

```python
import math

import jax
import jax.numpy as jnp
from jax import lax
from jax.sharding import PartitionSpec as P

L = 16


def phase_rows(q_coords, cell_coords):
    products = (
        q_coords[:, None, 0] * cell_coords[None, :, 0]
        + q_coords[:, None, 1] * cell_coords[None, :, 1]
        + q_coords[:, None, 2] * cell_coords[None, :, 2]
    )
    step = jnp.arange(4, dtype=jnp.float32) * (2.0 * math.pi / L)
    cos_table = jnp.cos(step).astype(jnp.bfloat16)
    sin_table = (-jnp.sin(step)).astype(jnp.bfloat16)
    bit0 = (products & 1) != 0
    bit1 = (products & 2) != 0
    bit2 = (products & 4) != 0
    bit3 = (products & 8) != 0
    real = jnp.where(bit1, jnp.where(bit0, cos_table[3], cos_table[2]), jnp.where(bit0, cos_table[1], cos_table[0]))
    imag = jnp.where(bit1, jnp.where(bit0, sin_table[3], sin_table[2]), jnp.where(bit0, sin_table[1], sin_table[0]))
    real, imag = jnp.where(bit2, imag, real), jnp.where(bit2, -real, imag)
    real, imag = jnp.where(bit3, -real, real), jnp.where(bit3, -imag, imag)
    return jnp.stack([real, imag], axis=1)


def twiddles(frames):
    inner = 16
    outer = frames // inner
    w = jnp.arange(frames, dtype=jnp.int32)
    a = jnp.arange(outer, dtype=jnp.int32)
    b = jnp.arange(inner, dtype=jnp.int32)
    coarse = (a[:, None] * w[None, :] % outer).astype(jnp.float32) * (2.0 * math.pi / outer)
    fine = (b[:, None] * w[None, :] % frames).astype(jnp.float32) * (2.0 * math.pi / frames)
    cos_c, sin_c = jnp.cos(coarse)[:, None, :], jnp.sin(coarse)[:, None, :]
    cos_f, sin_f = jnp.cos(fine)[None, :, :], jnp.sin(fine)[None, :, :]
    cosines = (cos_c * cos_f - sin_c * sin_f).reshape(frames, frames)
    sines = (sin_c * cos_f + cos_c * sin_f).reshape(frames, frames)
    return cosines, sines


def local(velocity, cell_coords, q_coords, eigvecs):
    n_tm = lax.axis_size("tm")
    n_cell = lax.axis_size("cell")
    n_dev = n_tm * n_cell
    cell_dev, frames_dev, branches = velocity.shape
    q_total = q_coords.shape[0]
    q_local = q_total // n_dev
    frames = frames_dev * n_tm
    frames_each = frames_dev // n_cell
    spread = velocity.reshape(cell_dev, n_cell, frames_each * branches)
    all_cells = lax.all_to_all(spread, "cell", split_axis=1, concat_axis=0, tiled=True)
    all_cells = all_cells.reshape(cell_dev * n_cell, frames_each * branches)
    all_coords = lax.all_gather(cell_coords, "cell", axis=0, tiled=True)
    table = phase_rows(q_coords, all_coords).reshape(2 * q_total, cell_dev * n_cell)
    modes = jnp.dot(table, all_cells, preferred_element_type=jnp.float32)
    modes = modes.astype(jnp.bfloat16).reshape(n_dev, q_local, 2, frames_each, branches)
    collected = lax.all_to_all(modes, ("tm", "cell"), split_axis=0, concat_axis=0, tiled=True)

    scale = 1.0 / math.sqrt(cell_dev * n_cell)
    e_real = eigvecs[:, 0] * scale
    e_imag = eigvecs[:, 1] * scale
    e_block = jnp.stack(
        [jnp.concatenate([e_real, -e_imag], axis=2), jnp.concatenate([e_imag, e_real], axis=2)],
        axis=1,
    )
    highest = lax.Precision.HIGHEST
    amplitude = jnp.einsum(
        "sjrfk,jrkc->jsfc", collected.astype(jnp.float32), e_block, precision=highest
    ).reshape(q_local, frames, 2 * branches)
    cosines, sines = twiddles(frames)
    basis = jnp.concatenate([cosines, sines], axis=1)
    projected = jnp.einsum("jts,tw->jsw", amplitude, basis, precision=highest)
    on_cos = projected[:, :, :frames]
    on_sin = projected[:, :, frames:]
    out_real = on_cos[:, :branches] + on_sin[:, branches:]
    out_imag = on_cos[:, branches:] - on_sin[:, :branches]
    return (out_real * out_real + out_imag * out_imag) / frames


def solution(mesh):
    in_specs = (P("cell", "tm", None), P("cell", None), P(), P(("tm", "cell"), None, None, None))
    out_specs = P(("tm", "cell"), None, None)
    return jax.shard_map(local, mesh=mesh, in_specs=in_specs, out_specs=out_specs, check_vma=False)
```

```python
import math

import jax
import jax.numpy as jnp
from jax import lax
from jax.sharding import PartitionSpec as P

L = 16


def phase_rows(q_coords, cell_code):
    code = cell_code.astype(jnp.int32)
    products = (
        q_coords[:, None, 0] * (code[None, :] // (L * L))
        + q_coords[:, None, 1] * (code[None, :] // L % L)
        + q_coords[:, None, 2] * (code[None, :] % L)
    )
    step = jnp.arange(4, dtype=jnp.float32) * (2.0 * math.pi / L)
    cos_table = jnp.cos(step).astype(jnp.bfloat16)
    sin_table = (-jnp.sin(step)).astype(jnp.bfloat16)
    bit0 = (products & 1) != 0
    bit1 = (products & 2) != 0
    bit2 = (products & 4) != 0
    bit3 = (products & 8) != 0
    real = jnp.where(bit1, jnp.where(bit0, cos_table[3], cos_table[2]), jnp.where(bit0, cos_table[1], cos_table[0]))
    imag = jnp.where(bit1, jnp.where(bit0, sin_table[3], sin_table[2]), jnp.where(bit0, sin_table[1], sin_table[0]))
    real, imag = jnp.where(bit2, imag, real), jnp.where(bit2, -real, imag)
    real, imag = jnp.where(bit3, -real, real), jnp.where(bit3, -imag, imag)
    return jnp.stack([real, imag], axis=0)


def twiddles(frames):
    inner = 16
    outer = frames // inner
    w = jnp.arange(frames, dtype=jnp.int32)
    a = jnp.arange(outer, dtype=jnp.int32)
    b = jnp.arange(inner, dtype=jnp.int32)
    coarse = (a[:, None] * w[None, :] % outer).astype(jnp.float32) * (2.0 * math.pi / outer)
    fine = (b[:, None] * w[None, :] % frames).astype(jnp.float32) * (2.0 * math.pi / frames)
    cos_c, sin_c = jnp.cos(coarse)[:, None, :], jnp.sin(coarse)[:, None, :]
    cos_f, sin_f = jnp.cos(fine)[None, :, :], jnp.sin(fine)[None, :, :]
    cosines = (cos_c * cos_f - sin_c * sin_f).reshape(frames, frames)
    sines = (sin_c * cos_f + cos_c * sin_f).reshape(frames, frames)
    return cosines, sines


def local(velocity, cell_coords, q_coords, eigvecs):
    n_tm = lax.axis_size("tm")
    n_cell = lax.axis_size("cell")
    n_dev = n_tm * n_cell
    cell_dev, frames_dev, branches = velocity.shape
    q_total = q_coords.shape[0]
    q_local = q_total // n_dev
    frames = frames_dev * n_tm
    frames_each = frames_dev // n_cell
    spread = velocity.reshape(cell_dev, n_cell, frames_each * branches)
    cell_code = (cell_coords[:, 0] * (L * L) + cell_coords[:, 1] * L + cell_coords[:, 2]).astype(jnp.float32)
    all_code = lax.all_gather(cell_code, "cell", axis=0, tiled=True)
    all_code, spread = lax.optimization_barrier((all_code, spread))
    all_cells = lax.all_to_all(spread, "cell", split_axis=1, concat_axis=0, tiled=True)
    all_cells = all_cells.reshape(cell_dev * n_cell, frames_each * branches)
    table = phase_rows(q_coords, all_code).reshape(2 * q_total, cell_dev * n_cell)
    modes = jnp.dot(table, all_cells, preferred_element_type=jnp.float32)
    modes = modes.astype(jnp.bfloat16).reshape(2, n_dev, q_local, frames_each, branches)
    collected = lax.all_to_all(modes, ("tm", "cell"), split_axis=1, concat_axis=1, tiled=True)

    scale = 1.0 / math.sqrt(cell_dev * n_cell)
    e_real = eigvecs[:, 0] * scale
    e_imag = eigvecs[:, 1] * scale
    e_block = jnp.stack(
        [jnp.concatenate([e_real, -e_imag], axis=2), jnp.concatenate([e_imag, e_real], axis=2)],
        axis=1,
    )
    highest = lax.Precision.HIGHEST
    amplitude = jnp.einsum(
        "rsjfk,jrkc->jsfc", collected.astype(jnp.float32), e_block, precision=highest
    ).reshape(q_local, frames, 2 * branches)
    cosines, sines = twiddles(frames)
    basis = jnp.concatenate([cosines, sines], axis=1)
    projected = jnp.einsum("jts,tw->jsw", amplitude, basis, precision=highest)
    on_cos = projected[:, :, :frames]
    on_sin = projected[:, :, frames:]
    out_real = on_cos[:, :branches] + on_sin[:, branches:]
    out_imag = on_cos[:, branches:] - on_sin[:, :branches]
    return (out_real * out_real + out_imag * out_imag) / frames


def solution(mesh):
    in_specs = (P("cell", "tm", None), P("cell", None), P(), P(("tm", "cell"), None, None, None))
    out_specs = P(("tm", "cell"), None, None)
    return jax.shard_map(local, mesh=mesh, in_specs=in_specs, out_specs=out_specs, check_vma=False)
```

```python
import math

import jax
import jax.numpy as jnp
from jax import lax
from jax.sharding import PartitionSpec as P

L = 16


def phase_rows(q_coords, cell_coords):
    products = (
        q_coords[:, None, 0] * cell_coords[None, :, 0]
        + q_coords[:, None, 1] * cell_coords[None, :, 1]
        + q_coords[:, None, 2] * cell_coords[None, :, 2]
    )
    step = jnp.arange(4, dtype=jnp.float32) * (2.0 * math.pi / L)
    cos_table = jnp.cos(step).astype(jnp.bfloat16)
    sin_table = (-jnp.sin(step)).astype(jnp.bfloat16)
    bit0 = (products & 1) != 0
    bit1 = (products & 2) != 0
    bit2 = (products & 4) != 0
    bit3 = (products & 8) != 0
    real = jnp.where(bit1, jnp.where(bit0, cos_table[3], cos_table[2]), jnp.where(bit0, cos_table[1], cos_table[0]))
    imag = jnp.where(bit1, jnp.where(bit0, sin_table[3], sin_table[2]), jnp.where(bit0, sin_table[1], sin_table[0]))
    real, imag = jnp.where(bit2, imag, real), jnp.where(bit2, -real, imag)
    real, imag = jnp.where(bit3, -real, real), jnp.where(bit3, -imag, imag)
    return real, imag


def twiddles(frames):
    inner = 16
    outer = frames // inner
    w = jnp.arange(frames, dtype=jnp.int32)
    a = jnp.arange(outer, dtype=jnp.int32)
    b = jnp.arange(inner, dtype=jnp.int32)
    coarse = (a[:, None] * w[None, :] % outer).astype(jnp.float32) * (2.0 * math.pi / outer)
    fine = (b[:, None] * w[None, :] % frames).astype(jnp.float32) * (2.0 * math.pi / frames)
    cos_c, sin_c = jnp.cos(coarse)[:, None, :], jnp.sin(coarse)[:, None, :]
    cos_f, sin_f = jnp.cos(fine)[None, :, :], jnp.sin(fine)[None, :, :]
    cosines = (cos_c * cos_f - sin_c * sin_f).reshape(frames, frames)
    sines = (sin_c * cos_f + cos_c * sin_f).reshape(frames, frames)
    return cosines, sines


def local(velocity, cell_coords, q_coords, eigvecs):
    n_tm = lax.axis_size("tm")
    n_cell = lax.axis_size("cell")
    cell_dev, frames_dev, branches = velocity.shape
    q_total = q_coords.shape[0]
    q_local = q_total // (n_tm * n_cell)
    frames = frames_dev * n_tm
    ordered_coords = (
        q_coords.reshape(n_tm, n_cell, q_local, 3).transpose(1, 0, 2, 3).reshape(q_total, 3)
    )
    cos_rows, sin_rows = phase_rows(ordered_coords, cell_coords)
    table = jnp.stack(
        [
            cos_rows.reshape(n_cell, n_tm * q_local, cell_dev),
            sin_rows.reshape(n_cell, n_tm * q_local, cell_dev),
        ],
        axis=1,
    ).reshape(2 * q_total, cell_dev)
    velocity_rows = velocity.reshape(cell_dev, frames_dev * branches)
    partial_term = jnp.dot(table, velocity_rows, preferred_element_type=jnp.float32)
    partial_term = partial_term.astype(jnp.bfloat16).reshape(
        n_cell, 2 * n_tm * q_local, frames_dev * branches
    )
    gathered = lax.all_to_all(partial_term, "cell", split_axis=0, concat_axis=0, tiled=True)
    summed = jnp.sum(gathered.astype(jnp.float32), axis=0).astype(jnp.bfloat16)
    blocks = summed.reshape(2, n_tm, q_local, frames_dev, branches)
    collected = lax.all_to_all(blocks, "tm", split_axis=1, concat_axis=3, tiled=True)
    collected = collected.reshape(2, q_local, frames, branches).astype(jnp.float32)

    scale = 1.0 / math.sqrt(cell_dev * n_cell)
    e_real = eigvecs[:, 0] * scale
    e_imag = eigvecs[:, 1] * scale
    e_block = jnp.stack(
        [jnp.concatenate([e_real, -e_imag], axis=2), jnp.concatenate([e_imag, e_real], axis=2)],
        axis=1,
    )
    highest = lax.Precision.HIGHEST
    amplitude = jnp.einsum("rjtk,jrks->jts", collected, e_block, precision=highest)
    cosines, sines = twiddles(frames)
    basis = jnp.concatenate([cosines, sines], axis=1)
    projected = jnp.einsum("jts,tw->jsw", amplitude, basis, precision=lax.Precision.HIGH)
    on_cos = projected[:, :, :frames]
    on_sin = projected[:, :, frames:]
    out_real = on_cos[:, :branches] + on_sin[:, branches:]
    out_imag = on_cos[:, branches:] - on_sin[:, :branches]
    return (out_real * out_real + out_imag * out_imag) / frames


def solution(mesh):
    in_specs = (P("cell", "tm", None), P("cell", None), P(), P(("tm", "cell"), None, None, None))
    out_specs = P(("tm", "cell"), None, None)
    return jax.shard_map(local, mesh=mesh, in_specs=in_specs, out_specs=out_specs, check_vma=False)
```

```python
import math

import jax
import jax.numpy as jnp
from jax import lax
from jax.sharding import PartitionSpec as P

L = 16


def phase_rows(q_coords, cell_coords):
    products = (
        q_coords[:, None, 0] * cell_coords[None, :, 0]
        + q_coords[:, None, 1] * cell_coords[None, :, 1]
        + q_coords[:, None, 2] * cell_coords[None, :, 2]
    ) % L
    angles = products.astype(jnp.float32) * (2.0 * math.pi / L)
    return jnp.cos(angles).astype(jnp.bfloat16), (-jnp.sin(angles)).astype(jnp.bfloat16)


def twiddles(frames):
    inner = 16
    outer = frames // inner
    w = jnp.arange(frames, dtype=jnp.int32)
    a = jnp.arange(outer, dtype=jnp.int32)
    b = jnp.arange(inner, dtype=jnp.int32)
    coarse = (a[:, None] * w[None, :] % outer).astype(jnp.float32) * (2.0 * math.pi / outer)
    fine = (b[:, None] * w[None, :] % frames).astype(jnp.float32) * (2.0 * math.pi / frames)
    cos_c, sin_c = jnp.cos(coarse)[:, None, :], jnp.sin(coarse)[:, None, :]
    cos_f, sin_f = jnp.cos(fine)[None, :, :], jnp.sin(fine)[None, :, :]
    cosines = (cos_c * cos_f - sin_c * sin_f).reshape(frames, frames)
    sines = (sin_c * cos_f + cos_c * sin_f).reshape(frames, frames)
    return cosines, sines


def local(velocity, cell_coords, q_coords, eigvecs):
    n_tm = lax.axis_size("tm")
    n_cell = lax.axis_size("cell")
    cell_dev, frames_dev, branches = velocity.shape
    q_total = q_coords.shape[0]
    q_local = q_total // (n_tm * n_cell)
    frames = frames_dev * n_tm
    ordered_coords = (
        q_coords.reshape(n_tm, n_cell, q_local, 3).transpose(1, 0, 2, 3).reshape(q_total, 3)
    )
    cos_rows, sin_rows = phase_rows(ordered_coords, cell_coords)
    table = jnp.stack(
        [
            cos_rows.reshape(n_cell, n_tm, q_local, cell_dev),
            sin_rows.reshape(n_cell, n_tm, q_local, cell_dev),
        ],
        axis=2,
    ).reshape(2 * q_total, cell_dev)
    velocity_rows = velocity.reshape(cell_dev, frames_dev * branches)
    partial_term = jnp.dot(table, velocity_rows, preferred_element_type=jnp.float32)
    partial_term = partial_term.astype(jnp.bfloat16).reshape(
        n_cell, 2 * n_tm * q_local, frames_dev * branches
    )
    gathered = lax.all_to_all(partial_term, "cell", split_axis=0, concat_axis=0, tiled=True)
    summed = jnp.sum(gathered.astype(jnp.float32), axis=0).astype(jnp.bfloat16)
    blocks = summed.reshape(n_tm, 2, q_local, frames_dev, branches)
    collected = lax.all_to_all(blocks, "tm", split_axis=0, concat_axis=0, tiled=True)
    collected = collected.astype(jnp.float32)

    scale = 1.0 / math.sqrt(cell_dev * n_cell)
    e_real = eigvecs[:, 0] * scale
    e_imag = eigvecs[:, 1] * scale
    e_block = jnp.stack(
        [jnp.concatenate([e_real, -e_imag], axis=2), jnp.concatenate([e_imag, e_real], axis=2)],
        axis=1,
    )
    highest = lax.Precision.HIGHEST
    amplitude = jnp.einsum("arjtk,jrks->jats", collected, e_block, precision=highest).reshape(
        q_local, frames, 2 * branches
    )
    cosines, sines = twiddles(frames)
    basis = jnp.concatenate([cosines, sines], axis=1)
    projected = jnp.einsum("jts,tw->jsw", amplitude, basis, precision=lax.Precision.HIGH)
    on_cos = projected[:, :, :frames]
    on_sin = projected[:, :, frames:]
    out_real = on_cos[:, :branches] + on_sin[:, branches:]
    out_imag = on_cos[:, branches:] - on_sin[:, :branches]
    return (out_real * out_real + out_imag * out_imag) / frames


def solution(mesh):
    in_specs = (P("cell", "tm", None), P("cell", None), P(), P(("tm", "cell"), None, None, None))
    out_specs = P(("tm", "cell"), None, None)
    return jax.shard_map(local, mesh=mesh, in_specs=in_specs, out_specs=out_specs, check_vma=False)
```

```python
import math

import jax
import jax.numpy as jnp
from jax import lax
from jax.sharding import PartitionSpec as P

L = 16


def twiddles(frames):
    inner = 16
    outer = frames // inner
    w = jnp.arange(frames, dtype=jnp.int32)
    a = jnp.arange(outer, dtype=jnp.int32)
    b = jnp.arange(inner, dtype=jnp.int32)
    coarse = (a[:, None] * w[None, :] % outer).astype(jnp.float32) * (2.0 * math.pi / outer)
    fine = (b[:, None] * w[None, :] % frames).astype(jnp.float32) * (2.0 * math.pi / frames)
    cos_c, sin_c = jnp.cos(coarse)[:, None, :], jnp.sin(coarse)[:, None, :]
    cos_f, sin_f = jnp.cos(fine)[None, :, :], jnp.sin(fine)[None, :, :]
    cosines = (cos_c * cos_f - sin_c * sin_f).reshape(frames, frames)
    sines = (sin_c * cos_f + cos_c * sin_f).reshape(frames, frames)
    return cosines, sines


def lattice_dft(on_lattice):
    high = lax.Precision.HIGH
    width = on_lattice.shape[1]
    k = jnp.arange(L, dtype=jnp.int32)
    angle = ((k[:, None] * k[None, :]) % L).astype(jnp.float32) * (2.0 * math.pi / L)
    w_re, w_im = jnp.cos(angle), -jnp.sin(angle)
    yz_re = (w_re[:, None, :, None] * w_re[None, :, None, :] - w_im[:, None, :, None] * w_im[None, :, None, :])
    yz_im = (w_re[:, None, :, None] * w_im[None, :, None, :] + w_im[:, None, :, None] * w_re[None, :, None, :])
    plane = jnp.stack([yz_re, yz_im]).reshape(2, L * L, L * L)
    grid = on_lattice.astype(jnp.float32).reshape(L, L * L, width)
    on_plane = jnp.einsum("rpm,xmf->rxpf", plane, grid, precision=high)
    line = jnp.stack(
        [jnp.stack([w_re, -w_im]), jnp.stack([w_im, w_re])]
    )
    full = jnp.einsum("rsax,sxpf->rapf", line, on_plane, precision=high)
    return full.reshape(2, L * L * L, width)


def local(velocity, cell_coords, q_coords, eigvecs):
    n_tm = lax.axis_size("tm")
    n_cell = lax.axis_size("cell")
    n_dev = n_tm * n_cell
    cell_dev, frames_dev, branches = velocity.shape
    q_total = q_coords.shape[0]
    q_local = q_total // n_dev
    frames = frames_dev * n_tm
    frames_each = frames_dev // n_cell
    width = frames_each * branches
    spread = velocity.reshape(cell_dev, n_cell, width)
    position = jnp.broadcast_to(cell_coords.astype(jnp.bfloat16)[:, None, :], (cell_dev, n_cell, 3))
    payload = jnp.concatenate([spread, position], axis=2)
    received = lax.all_to_all(payload, "cell", split_axis=1, concat_axis=0, tiled=True)
    received = received.reshape(cell_dev * n_cell, width + 3)
    where = received[:, width:].astype(jnp.int32)
    lattice = where[:, 0] * (L * L) + where[:, 1] * L + where[:, 2]
    order = jnp.argsort(lattice)
    on_lattice = jnp.take(received[:, :width], order, axis=0)
    full = lattice_dft(on_lattice)
    q_index = q_coords[:, 0] * (L * L) + q_coords[:, 1] * L + q_coords[:, 2]
    modes = jnp.take(full, q_index, axis=1).astype(jnp.bfloat16)
    modes = modes.reshape(2, n_dev, q_local, frames_each, branches)
    collected = lax.all_to_all(modes, ("tm", "cell"), split_axis=1, concat_axis=1, tiled=True)

    scale = 1.0 / math.sqrt(cell_dev * n_cell)
    e_real = eigvecs[:, 0] * scale
    e_imag = eigvecs[:, 1] * scale
    e_block = jnp.stack(
        [jnp.concatenate([e_real, -e_imag], axis=2), jnp.concatenate([e_imag, e_real], axis=2)],
        axis=1,
    )
    highest = lax.Precision.HIGHEST
    amplitude = jnp.einsum(
        "rsjfk,jrkc->jsfc", collected.astype(jnp.float32), e_block, precision=highest
    ).reshape(q_local, frames, 2 * branches)
    cosines, sines = twiddles(frames)
    basis = jnp.concatenate([cosines, sines], axis=1)
    projected = jnp.einsum("jts,tw->jsw", amplitude, basis, precision=lax.Precision.HIGH)
    on_cos = projected[:, :, :frames]
    on_sin = projected[:, :, frames:]
    out_real = on_cos[:, :branches] + on_sin[:, branches:]
    out_imag = on_cos[:, branches:] - on_sin[:, :branches]
    return (out_real * out_real + out_imag * out_imag) / frames


def solution(mesh):
    in_specs = (P("cell", "tm", None), P("cell", None), P(), P(("tm", "cell"), None, None, None))
    out_specs = P(("tm", "cell"), None, None)
    return jax.shard_map(local, mesh=mesh, in_specs=in_specs, out_specs=out_specs, check_vma=False)
```

```python
import math

import jax
import jax.numpy as jnp
from jax import lax
from jax.sharding import PartitionSpec as P

L = 16


def phase_rows(q_coords, cell_coords):
    products = (
        q_coords[0][:, None] * cell_coords[None, :, 0]
        + q_coords[1][:, None] * cell_coords[None, :, 1]
        + q_coords[2][:, None] * cell_coords[None, :, 2]
    ) % L
    angles = products.astype(jnp.float32) * (2.0 * math.pi / L)
    return jnp.cos(angles).astype(jnp.bfloat16), (-jnp.sin(angles)).astype(jnp.bfloat16)


def twiddles(frames):
    inner = 16
    outer = frames // inner
    w = jnp.arange(frames, dtype=jnp.int32)
    a = jnp.arange(outer, dtype=jnp.int32)
    b = jnp.arange(inner, dtype=jnp.int32)
    coarse = (a[:, None] * w[None, :] % outer).astype(jnp.float32) * (2.0 * math.pi / outer)
    fine = (b[:, None] * w[None, :] % frames).astype(jnp.float32) * (2.0 * math.pi / frames)
    cos_c, sin_c = jnp.cos(coarse)[:, None, :], jnp.sin(coarse)[:, None, :]
    cos_f, sin_f = jnp.cos(fine)[None, :, :], jnp.sin(fine)[None, :, :]
    cosines = (cos_c * cos_f - sin_c * sin_f).reshape(frames, frames)
    sines = (sin_c * cos_f + cos_c * sin_f).reshape(frames, frames)
    return cosines, sines


def local(velocity, cell_coords, q_coords, eigvecs):
    n_tm = lax.axis_size("tm")
    n_cell = lax.axis_size("cell")
    cell_dev, frames_dev, branches = velocity.shape
    q_total = q_coords.shape[0]
    q_local = q_total // (n_tm * n_cell)
    frames = frames_dev * n_tm
    ordered_coords = [
        q_coords[:, d].reshape(n_tm, n_cell, q_local).transpose(1, 0, 2).reshape(q_total)
        for d in range(3)
    ]
    cos_rows, sin_rows = phase_rows(ordered_coords, cell_coords)
    table = jnp.stack(
        [
            cos_rows.reshape(n_cell, n_tm * q_local, cell_dev),
            sin_rows.reshape(n_cell, n_tm * q_local, cell_dev),
        ],
        axis=1,
    ).reshape(2 * q_total, cell_dev)
    velocity_rows = velocity.reshape(cell_dev, frames_dev * branches)
    partial_term = jnp.dot(table, velocity_rows, preferred_element_type=jnp.float32)
    partial_term = partial_term.astype(jnp.bfloat16).reshape(
        n_cell, 2 * n_tm * q_local, frames_dev * branches
    )
    gathered = lax.all_to_all(partial_term, "cell", split_axis=0, concat_axis=0, tiled=True)
    summed = jnp.sum(gathered.astype(jnp.float32), axis=0).astype(jnp.bfloat16)
    blocks = summed.reshape(2, n_tm, q_local, frames_dev, branches).transpose(1, 0, 2, 3, 4)
    collected = lax.all_to_all(blocks, "tm", split_axis=0, concat_axis=0, tiled=True)
    collected = collected.astype(jnp.float32)

    scale = 1.0 / math.sqrt(cell_dev * n_cell)
    e_real = eigvecs[:, 0] * scale
    e_imag = eigvecs[:, 1] * scale
    e_block = jnp.stack(
        [jnp.concatenate([e_real, -e_imag], axis=2), jnp.concatenate([e_imag, e_real], axis=2)],
        axis=1,
    )
    highest = lax.Precision.HIGHEST
    amplitude = jnp.einsum("arjtk,jrks->jats", collected, e_block, precision=highest).reshape(
        q_local, frames, 2 * branches
    )
    cosines, sines = twiddles(frames)
    basis = jnp.concatenate([cosines, sines], axis=1)
    projected = jnp.einsum("jts,tw->jsw", amplitude, basis, precision=lax.Precision.HIGH)
    on_cos = projected[:, :, :frames]
    on_sin = projected[:, :, frames:]
    out_real = on_cos[:, :branches] + on_sin[:, branches:]
    out_imag = on_cos[:, branches:] - on_sin[:, :branches]
    return (out_real * out_real + out_imag * out_imag) / frames


def solution(mesh):
    in_specs = (P("cell", "tm", None), P("cell", None), P(), P(("tm", "cell"), None, None, None))
    out_specs = P(("tm", "cell"), None, None)
    return jax.shard_map(local, mesh=mesh, in_specs=in_specs, out_specs=out_specs, check_vma=False)
```

```python
import math

import jax
import jax.numpy as jnp
from jax import lax
from jax.experimental import pallas as pl
from jax.sharding import PartitionSpec as P
import numpy as np

L = 16


def quarter_tables():
    step = np.arange(4, dtype=np.float32) * np.float32(2.0 * math.pi / L)
    cos_k = np.cos(step).astype(jnp.bfloat16).astype(np.float32)
    sin_k = (-np.sin(step)).astype(jnp.bfloat16).astype(np.float32)
    return [float(v) for v in cos_k], [float(v) for v in sin_k]


def phase_sum_kernel(qx_ref, qy_ref, qz_ref, cx_ref, cy_ref, cz_ref, v_ref, o_ref):
    cos_k, sin_k = quarter_tables()
    m = (qx_ref[0] * cx_ref[...] + qy_ref[0] * cy_ref[...] + qz_ref[0] * cz_ref[...]) & (L - 1)
    bit0 = (m & 1) != 0
    bit1 = (m & 2) != 0
    bit2 = (m & 4) != 0
    bit3 = (m & 8) != 0
    real = jnp.where(bit1, jnp.where(bit0, cos_k[3], cos_k[2]), jnp.where(bit0, cos_k[1], cos_k[0]))
    imag = jnp.where(bit1, jnp.where(bit0, sin_k[3], sin_k[2]), jnp.where(bit0, sin_k[1], sin_k[0]))
    real, imag = jnp.where(bit2, imag, real), jnp.where(bit2, -real, imag)
    real, imag = jnp.where(bit3, -real, real), jnp.where(bit3, -imag, imag)
    v = v_ref[...]
    o_ref[0, 0] = jnp.dot(real.astype(jnp.bfloat16), v, preferred_element_type=jnp.float32).astype(o_ref.dtype)
    o_ref[0, 1] = jnp.dot(imag.astype(jnp.bfloat16), v, preferred_element_type=jnp.float32).astype(o_ref.dtype)


def phase_sums(q_columns, cell_coords, velocity_rows, groups):
    q_total = q_columns[0].shape[0]
    rows = q_total // groups
    cells, width = velocity_rows.shape
    q_in = [col.reshape(groups, rows, 1) for col in q_columns]
    c_in = [cell_coords[:, d].reshape(1, cells) for d in range(3)]
    q_spec = pl.BlockSpec((1, rows, 1), lambda i: (i, 0, 0))
    c_spec = pl.BlockSpec((1, cells), lambda i: (0, 0))
    return pl.pallas_call(
        phase_sum_kernel,
        grid=(groups,),
        in_specs=[q_spec] * 3 + [c_spec] * 3 + [pl.BlockSpec((cells, width), lambda i: (0, 0))],
        out_specs=pl.BlockSpec((1, 2, rows, width), lambda i: (i, 0, 0, 0)),
        out_shape=jax.ShapeDtypeStruct((groups, 2, rows, width), jnp.bfloat16),
        cost_estimate=pl.CostEstimate(
            flops=4 * q_total * cells * width,
            transcendentals=0,
            bytes_accessed=2 * cells * width + 4 * q_total * width,
        ),
    )(*q_in, *c_in, velocity_rows)


def twiddles(frames):
    inner = 16
    outer = frames // inner
    w = jnp.arange(frames, dtype=jnp.int32)
    a = jnp.arange(outer, dtype=jnp.int32)
    b = jnp.arange(inner, dtype=jnp.int32)
    coarse = (a[:, None] * w[None, :] % outer).astype(jnp.float32) * (2.0 * math.pi / outer)
    fine = (b[:, None] * w[None, :] % frames).astype(jnp.float32) * (2.0 * math.pi / frames)
    cos_c, sin_c = jnp.cos(coarse)[:, None, :], jnp.sin(coarse)[:, None, :]
    cos_f, sin_f = jnp.cos(fine)[None, :, :], jnp.sin(fine)[None, :, :]
    cosines = (cos_c * cos_f - sin_c * sin_f).reshape(frames, frames)
    sines = (sin_c * cos_f + cos_c * sin_f).reshape(frames, frames)
    return cosines, sines


def local(velocity, cell_coords, q_coords, eigvecs):
    n_tm = lax.axis_size("tm")
    n_cell = lax.axis_size("cell")
    cell_dev, frames_dev, branches = velocity.shape
    q_total = q_coords.shape[0]
    q_local = q_total // (n_tm * n_cell)
    frames = frames_dev * n_tm
    ordered_coords = [
        q_coords[:, d].reshape(n_tm, n_cell, q_local).transpose(1, 0, 2).reshape(q_total)
        for d in range(3)
    ]
    velocity_rows = velocity.reshape(cell_dev, frames_dev * branches)
    partial_term = phase_sums(ordered_coords, cell_coords, velocity_rows, n_cell).reshape(
        n_cell, 2 * n_tm * q_local, frames_dev * branches
    )
    gathered = lax.all_to_all(partial_term, "cell", split_axis=0, concat_axis=0, tiled=True)
    summed = jnp.sum(gathered.astype(jnp.float32), axis=0).astype(jnp.bfloat16)
    blocks = summed.reshape(2, n_tm, q_local, frames_dev, branches).transpose(1, 0, 2, 3, 4)
    collected = lax.all_to_all(blocks, "tm", split_axis=0, concat_axis=0, tiled=True)
    collected = collected.astype(jnp.float32)

    scale = 1.0 / math.sqrt(cell_dev * n_cell)
    e_real = eigvecs[:, 0] * scale
    e_imag = eigvecs[:, 1] * scale
    e_block = jnp.stack(
        [jnp.concatenate([e_real, -e_imag], axis=2), jnp.concatenate([e_imag, e_real], axis=2)],
        axis=1,
    )
    highest = lax.Precision.HIGHEST
    amplitude = jnp.einsum("arjtk,jrks->jats", collected, e_block, precision=highest).reshape(
        q_local, frames, 2 * branches
    )
    cosines, sines = twiddles(frames)
    basis = jnp.concatenate([cosines, sines], axis=1)
    projected = jnp.einsum("jts,tw->jsw", amplitude, basis, precision=lax.Precision.HIGH)
    on_cos = projected[:, :, :frames]
    on_sin = projected[:, :, frames:]
    out_real = on_cos[:, :branches] + on_sin[:, branches:]
    out_imag = on_cos[:, branches:] - on_sin[:, :branches]
    return (out_real * out_real + out_imag * out_imag) / frames


def solution(mesh):
    in_specs = (P("cell", "tm", None), P("cell", None), P(), P(("tm", "cell"), None, None, None))
    out_specs = P(("tm", "cell"), None, None)
    return jax.shard_map(local, mesh=mesh, in_specs=in_specs, out_specs=out_specs, check_vma=False)
```

```python
import math

import jax
import jax.numpy as jnp
from jax import lax
from jax.experimental import pallas as pl
from jax.sharding import PartitionSpec as P
import numpy as np

L = 16


def quarter_tables():
    step = np.arange(4, dtype=np.float32) * np.float32(2.0 * math.pi / L)
    cos_k = np.cos(step).astype(jnp.bfloat16).astype(np.float32)
    sin_k = (-np.sin(step)).astype(jnp.bfloat16).astype(np.float32)
    return [float(v) for v in cos_k], [float(v) for v in sin_k]


def phase_sum_kernel(c_ref, q_ref, vt_ref, o_ref):
    cos_k, sin_k = quarter_tables()
    dots = jnp.dot(c_ref[...], q_ref[0], preferred_element_type=jnp.float32)
    m = dots.astype(jnp.int32) & (L - 1)
    bit0 = (m & 1) != 0
    bit1 = (m & 2) != 0
    bit2 = (m & 4) != 0
    bit3 = (m & 8) != 0
    real = jnp.where(bit1, jnp.where(bit0, cos_k[3], cos_k[2]), jnp.where(bit0, cos_k[1], cos_k[0]))
    imag = jnp.where(bit1, jnp.where(bit0, sin_k[3], sin_k[2]), jnp.where(bit0, sin_k[1], sin_k[0]))
    real, imag = jnp.where(bit2, imag, real), jnp.where(bit2, -real, imag)
    real, imag = jnp.where(bit3, -real, real), jnp.where(bit3, -imag, imag)
    column = lax.broadcasted_iota(jnp.int32, m.shape, 1)
    phase = jnp.where(column < m.shape[1] // 2, real, imag).astype(jnp.bfloat16)
    o_ref[0] = jnp.dot(vt_ref[...], phase, preferred_element_type=jnp.float32).astype(o_ref.dtype)


def phase_sums(q_columns, cell_coords, velocity_t):
    groups, _, rows = q_columns.shape
    width, cells = velocity_t.shape
    pad = 8
    c_in = jnp.pad(cell_coords, ((0, 0), (0, pad - 3))).astype(jnp.bfloat16)
    q_in = jnp.pad(jnp.concatenate([q_columns, q_columns], axis=2), ((0, 0), (0, pad - 3), (0, 0)))
    q_in = q_in.astype(jnp.bfloat16)
    return pl.pallas_call(
        phase_sum_kernel,
        grid=(groups,),
        in_specs=[
            pl.BlockSpec((cells, pad), lambda i: (0, 0)),
            pl.BlockSpec((1, pad, 2 * rows), lambda i: (i, 0, 0)),
            pl.BlockSpec((width, cells), lambda i: (0, 0)),
        ],
        out_specs=pl.BlockSpec((1, width, 2 * rows), lambda i: (i, 0, 0)),
        out_shape=jax.ShapeDtypeStruct((groups, width, 2 * rows), jnp.bfloat16),
        cost_estimate=pl.CostEstimate(
            flops=4 * groups * rows * cells * width,
            transcendentals=0,
            bytes_accessed=2 * cells * width + 4 * groups * rows * width,
        ),
    )(c_in, q_in, velocity_t)


def twiddles(frames):
    inner = 16
    outer = frames // inner
    w = jnp.arange(frames, dtype=jnp.int32)
    a = jnp.arange(outer, dtype=jnp.int32)
    b = jnp.arange(inner, dtype=jnp.int32)
    coarse = (a[:, None] * w[None, :] % outer).astype(jnp.float32) * (2.0 * math.pi / outer)
    fine = (b[:, None] * w[None, :] % frames).astype(jnp.float32) * (2.0 * math.pi / frames)
    cos_c, sin_c = jnp.cos(coarse)[:, None, :], jnp.sin(coarse)[:, None, :]
    cos_f, sin_f = jnp.cos(fine)[None, :, :], jnp.sin(fine)[None, :, :]
    cosines = (cos_c * cos_f - sin_c * sin_f).reshape(frames, frames)
    sines = (sin_c * cos_f + cos_c * sin_f).reshape(frames, frames)
    return cosines, sines


def local(velocity, cell_coords, q_coords, eigvecs):
    n_tm = lax.axis_size("tm")
    n_cell = lax.axis_size("cell")
    cell_dev, frames_dev, branches = velocity.shape
    q_total = q_coords.shape[0]
    q_local = q_total // (n_tm * n_cell)
    frames = frames_dev * n_tm
    q_columns = q_coords.reshape(n_tm, n_cell, q_local, 3).transpose(1, 3, 0, 2)
    q_columns = q_columns.reshape(n_cell, 3, n_tm * q_local)
    velocity_t = velocity.reshape(cell_dev, frames_dev * branches).T
    partial_term = phase_sums(q_columns, cell_coords, velocity_t)
    gathered = lax.all_to_all(partial_term, "cell", split_axis=0, concat_axis=0, tiled=True)
    summed = jnp.sum(gathered.astype(jnp.float32), axis=0).astype(jnp.bfloat16)
    blocks = summed.reshape(frames_dev, branches, 2, n_tm, q_local).transpose(3, 2, 4, 0, 1)
    collected = lax.all_to_all(blocks, "tm", split_axis=0, concat_axis=0, tiled=True)
    collected = collected.astype(jnp.float32)

    scale = 1.0 / math.sqrt(cell_dev * n_cell)
    e_real = eigvecs[:, 0] * scale
    e_imag = eigvecs[:, 1] * scale
    e_block = jnp.stack(
        [jnp.concatenate([e_real, -e_imag], axis=2), jnp.concatenate([e_imag, e_real], axis=2)],
        axis=1,
    )
    highest = lax.Precision.HIGHEST
    amplitude = jnp.einsum("arjtk,jrks->jats", collected, e_block, precision=highest).reshape(
        q_local, frames, 2 * branches
    )
    cosines, sines = twiddles(frames)
    basis = jnp.concatenate([cosines, sines], axis=1)
    projected = jnp.einsum("jts,tw->jsw", amplitude, basis, precision=lax.Precision.HIGH)
    on_cos = projected[:, :, :frames]
    on_sin = projected[:, :, frames:]
    out_real = on_cos[:, :branches] + on_sin[:, branches:]
    out_imag = on_cos[:, branches:] - on_sin[:, :branches]
    return (out_real * out_real + out_imag * out_imag) / frames


def solution(mesh):
    in_specs = (P("cell", "tm", None), P("cell", None), P(), P(("tm", "cell"), None, None, None))
    out_specs = P(("tm", "cell"), None, None)
    return jax.shard_map(local, mesh=mesh, in_specs=in_specs, out_specs=out_specs, check_vma=False)
```

```python
import math

import jax
import jax.numpy as jnp
from jax import lax
from jax.experimental import pallas as pl
from jax.experimental.pallas import tpu as pltpu
from jax.sharding import PartitionSpec as P
import numpy as np

L = 16


def quarter_tables():
    step = np.arange(4, dtype=np.float32) * np.float32(2.0 * math.pi / L)
    cos_k = np.cos(step).astype(jnp.bfloat16).astype(np.float32)
    sin_k = (-np.sin(step)).astype(jnp.bfloat16).astype(np.float32)
    return [float(v) for v in cos_k], [float(v) for v in sin_k]


def phase_sum_kernel(c_ref, q_ref, vt_ref, o_ref, phase_ref):
    groups, _, group_width = o_ref.shape

    @pl.when(pl.program_id(0) == 0)
    def _():
        cos_k, sin_k = quarter_tables()
        dots = jnp.dot(c_ref[...], q_ref[...], preferred_element_type=jnp.float32)
        m = dots.astype(jnp.int32) & (L - 1)
        bit0 = (m & 1) != 0
        bit1 = (m & 2) != 0
        bit2 = (m & 4) != 0
        bit3 = (m & 8) != 0
        real = jnp.where(bit1, jnp.where(bit0, cos_k[3], cos_k[2]), jnp.where(bit0, cos_k[1], cos_k[0]))
        imag = jnp.where(bit1, jnp.where(bit0, sin_k[3], sin_k[2]), jnp.where(bit0, sin_k[1], sin_k[0]))
        real, imag = jnp.where(bit2, imag, real), jnp.where(bit2, -real, imag)
        real, imag = jnp.where(bit3, -real, real), jnp.where(bit3, -imag, imag)
        column = lax.broadcasted_iota(jnp.int32, m.shape, 1) % group_width
        phase_ref[...] = jnp.where(column < group_width // 2, real, imag).astype(jnp.bfloat16)

    sums = jnp.dot(vt_ref[...], phase_ref[...], preferred_element_type=jnp.float32)
    for g in range(groups):
        o_ref[g] = sums[:, g * group_width:(g + 1) * group_width].astype(o_ref.dtype)


def phase_sums(q_columns, cell_coords, velocity_t):
    groups, _, rows = q_columns.shape
    width, cells = velocity_t.shape
    pad = 8
    block = 256
    c_in = jnp.pad(cell_coords, ((0, 0), (0, pad - 3))).astype(jnp.bfloat16)
    q_in = jnp.concatenate([q_columns, q_columns], axis=2).transpose(1, 0, 2).reshape(3, groups * 2 * rows)
    q_in = jnp.pad(q_in, ((0, pad - 3), (0, 0))).astype(jnp.bfloat16)
    return pl.pallas_call(
        phase_sum_kernel,
        grid=(width // block,),
        in_specs=[
            pl.BlockSpec((cells, pad), lambda i: (0, 0)),
            pl.BlockSpec((pad, groups * 2 * rows), lambda i: (0, 0)),
            pl.BlockSpec((block, cells), lambda i: (i, 0)),
        ],
        out_specs=pl.BlockSpec((groups, block, 2 * rows), lambda i: (0, i, 0)),
        out_shape=jax.ShapeDtypeStruct((groups, width, 2 * rows), jnp.bfloat16),
        scratch_shapes=[pltpu.VMEM((cells, groups * 2 * rows), jnp.bfloat16)],
        cost_estimate=pl.CostEstimate(
            flops=4 * groups * rows * cells * width,
            transcendentals=0,
            bytes_accessed=2 * cells * width + 4 * groups * rows * width,
        ),
    )(c_in, q_in, velocity_t)


def twiddles(frames):
    inner = 16
    outer = frames // inner
    w = jnp.arange(frames, dtype=jnp.int32)
    a = jnp.arange(outer, dtype=jnp.int32)
    b = jnp.arange(inner, dtype=jnp.int32)
    coarse = (a[:, None] * w[None, :] % outer).astype(jnp.float32) * (2.0 * math.pi / outer)
    fine = (b[:, None] * w[None, :] % frames).astype(jnp.float32) * (2.0 * math.pi / frames)
    cos_c, sin_c = jnp.cos(coarse)[:, None, :], jnp.sin(coarse)[:, None, :]
    cos_f, sin_f = jnp.cos(fine)[None, :, :], jnp.sin(fine)[None, :, :]
    cosines = (cos_c * cos_f - sin_c * sin_f).reshape(frames, frames)
    sines = (sin_c * cos_f + cos_c * sin_f).reshape(frames, frames)
    return cosines, sines


def local(velocity, cell_coords, q_coords, eigvecs):
    n_tm = lax.axis_size("tm")
    n_cell = lax.axis_size("cell")
    cell_dev, frames_dev, branches = velocity.shape
    q_total = q_coords.shape[0]
    q_local = q_total // (n_tm * n_cell)
    frames = frames_dev * n_tm
    q_columns = q_coords.reshape(n_tm, n_cell, q_local, 3).transpose(1, 3, 0, 2)
    q_columns = q_columns.reshape(n_cell, 3, n_tm * q_local)
    velocity_t = velocity.reshape(cell_dev, frames_dev * branches).T
    partial_term = phase_sums(q_columns, cell_coords, velocity_t)
    gathered = lax.all_to_all(partial_term, "cell", split_axis=0, concat_axis=0, tiled=True)
    summed = jnp.sum(gathered.astype(jnp.float32), axis=0).astype(jnp.bfloat16)
    blocks = summed.reshape(frames_dev, branches, 2, n_tm, q_local).transpose(3, 2, 4, 0, 1)
    collected = lax.all_to_all(blocks, "tm", split_axis=0, concat_axis=0, tiled=True)
    collected = collected.astype(jnp.float32)

    scale = 1.0 / math.sqrt(cell_dev * n_cell)
    e_real = eigvecs[:, 0] * scale
    e_imag = eigvecs[:, 1] * scale
    e_block = jnp.stack(
        [jnp.concatenate([e_real, -e_imag], axis=2), jnp.concatenate([e_imag, e_real], axis=2)],
        axis=1,
    )
    highest = lax.Precision.HIGHEST
    amplitude = jnp.einsum("arjtk,jrks->jats", collected, e_block, precision=highest).reshape(
        q_local, frames, 2 * branches
    )
    cosines, sines = twiddles(frames)
    basis = jnp.concatenate([cosines, sines], axis=1)
    projected = jnp.einsum("jts,tw->jsw", amplitude, basis, precision=lax.Precision.HIGH)
    on_cos = projected[:, :, :frames]
    on_sin = projected[:, :, frames:]
    out_real = on_cos[:, :branches] + on_sin[:, branches:]
    out_imag = on_cos[:, branches:] - on_sin[:, :branches]
    return (out_real * out_real + out_imag * out_imag) / frames


def solution(mesh):
    in_specs = (P("cell", "tm", None), P("cell", None), P(), P(("tm", "cell"), None, None, None))
    out_specs = P(("tm", "cell"), None, None)
    return jax.shard_map(local, mesh=mesh, in_specs=in_specs, out_specs=out_specs, check_vma=False)
```

```python
import math

import jax
import jax.numpy as jnp
from jax import lax
from jax.experimental import pallas as pl
from jax.experimental.pallas import tpu as pltpu
from jax.sharding import PartitionSpec as P
import numpy as np

L = 16


def quarter_tables():
    step = np.arange(4, dtype=np.float32) * np.float32(2.0 * math.pi / L)
    cos_k = np.cos(step).astype(jnp.bfloat16).astype(np.float32)
    sin_k = (-np.sin(step)).astype(jnp.bfloat16).astype(np.float32)
    return [float(v) for v in cos_k], [float(v) for v in sin_k]


def phase_block(c_ref, q_ref, block, group_width):
    cos_k, sin_k = quarter_tables()
    dots = jnp.dot(c_ref[...], q_ref[block], preferred_element_type=jnp.float32)
    m = dots.astype(jnp.int32) & (L - 1)
    bit0 = (m & 1) != 0
    bit1 = (m & 2) != 0
    bit2 = (m & 4) != 0
    bit3 = (m & 8) != 0
    real = jnp.where(bit1, jnp.where(bit0, cos_k[3], cos_k[2]), jnp.where(bit0, cos_k[1], cos_k[0]))
    imag = jnp.where(bit1, jnp.where(bit0, sin_k[3], sin_k[2]), jnp.where(bit0, sin_k[1], sin_k[0]))
    real, imag = jnp.where(bit2, imag, real), jnp.where(bit2, -real, imag)
    real, imag = jnp.where(bit3, -real, real), jnp.where(bit3, -imag, imag)
    column = lax.broadcasted_iota(jnp.int32, m.shape, 1) % group_width
    return jnp.where(column < group_width // 2, real, imag).astype(jnp.bfloat16)


def phase_sum_kernel(c_ref, q_ref, vt_ref, o_ref, phase_ref):
    per_step, _, group_width = o_ref.shape
    step = pl.program_id(0)
    steps = pl.num_programs(0)
    slot = step % 2

    @pl.when(step == 0)
    def _():
        phase_ref[0] = phase_block(c_ref, q_ref, 0, group_width)

    @pl.when(step + 1 < steps)
    def _():
        phase_ref[1 - slot] = phase_block(c_ref, q_ref, step + 1, group_width)

    sums = jnp.dot(vt_ref[...], phase_ref[slot], preferred_element_type=jnp.float32)
    for g in range(per_step):
        o_ref[g] = sums[:, g * group_width:(g + 1) * group_width].astype(o_ref.dtype)


def phase_sums(q_columns, cell_coords, velocity_t):
    groups, _, rows = q_columns.shape
    width, cells = velocity_t.shape
    pad = 8
    per_step = 2
    steps = groups // per_step
    block_width = per_step * 2 * rows
    c_in = jnp.pad(cell_coords, ((0, 0), (0, pad - 3))).astype(jnp.bfloat16)
    q_in = jnp.concatenate([q_columns, q_columns], axis=2).transpose(1, 0, 2).reshape(3, steps, block_width)
    q_in = jnp.pad(q_in, ((0, pad - 3), (0, 0), (0, 0))).transpose(1, 0, 2).astype(jnp.bfloat16)
    return pl.pallas_call(
        phase_sum_kernel,
        grid=(steps,),
        in_specs=[
            pl.BlockSpec((cells, pad), lambda i: (0, 0)),
            pl.BlockSpec((steps, pad, block_width), lambda i: (0, 0, 0)),
            pl.BlockSpec((width, cells), lambda i: (0, 0)),
        ],
        out_specs=pl.BlockSpec((per_step, width, 2 * rows), lambda i: (i, 0, 0)),
        out_shape=jax.ShapeDtypeStruct((groups, width, 2 * rows), jnp.bfloat16),
        scratch_shapes=[pltpu.VMEM((2, cells, block_width), jnp.bfloat16)],
        cost_estimate=pl.CostEstimate(
            flops=4 * groups * rows * cells * width,
            transcendentals=0,
            bytes_accessed=2 * cells * width + 4 * groups * rows * width,
        ),
    )(c_in, q_in, velocity_t)


def twiddles(frames):
    inner = 16
    outer = frames // inner
    w = jnp.arange(frames, dtype=jnp.int32)
    a = jnp.arange(outer, dtype=jnp.int32)
    b = jnp.arange(inner, dtype=jnp.int32)
    coarse = (a[:, None] * w[None, :] % outer).astype(jnp.float32) * (2.0 * math.pi / outer)
    fine = (b[:, None] * w[None, :] % frames).astype(jnp.float32) * (2.0 * math.pi / frames)
    cos_c, sin_c = jnp.cos(coarse)[:, None, :], jnp.sin(coarse)[:, None, :]
    cos_f, sin_f = jnp.cos(fine)[None, :, :], jnp.sin(fine)[None, :, :]
    cosines = (cos_c * cos_f - sin_c * sin_f).reshape(frames, frames)
    sines = (sin_c * cos_f + cos_c * sin_f).reshape(frames, frames)
    return cosines, sines


def local(velocity, cell_coords, q_coords, eigvecs):
    n_tm = lax.axis_size("tm")
    n_cell = lax.axis_size("cell")
    cell_dev, frames_dev, branches = velocity.shape
    q_total = q_coords.shape[0]
    q_local = q_total // (n_tm * n_cell)
    frames = frames_dev * n_tm
    q_columns = q_coords.reshape(n_tm, n_cell, q_local, 3).transpose(1, 3, 0, 2)
    q_columns = q_columns.reshape(n_cell, 3, n_tm * q_local)
    velocity_t = velocity.reshape(cell_dev, frames_dev * branches).T
    partial_term = phase_sums(q_columns, cell_coords, velocity_t)
    gathered = lax.all_to_all(partial_term, "cell", split_axis=0, concat_axis=0, tiled=True)
    summed = jnp.sum(gathered.astype(jnp.float32), axis=0).astype(jnp.bfloat16)
    blocks = summed.reshape(frames_dev, branches, 2, n_tm, q_local).transpose(3, 2, 4, 0, 1)
    collected = lax.all_to_all(blocks, "tm", split_axis=0, concat_axis=0, tiled=True)
    collected = collected.astype(jnp.float32)

    scale = 1.0 / math.sqrt(cell_dev * n_cell)
    e_real = eigvecs[:, 0] * scale
    e_imag = eigvecs[:, 1] * scale
    e_block = jnp.stack(
        [jnp.concatenate([e_real, -e_imag], axis=2), jnp.concatenate([e_imag, e_real], axis=2)],
        axis=1,
    )
    highest = lax.Precision.HIGHEST
    amplitude = jnp.einsum("arjtk,jrks->jats", collected, e_block, precision=highest).reshape(
        q_local, frames, 2 * branches
    )
    cosines, sines = twiddles(frames)
    basis = jnp.concatenate([cosines, sines], axis=1)
    projected = jnp.einsum("jts,tw->jsw", amplitude, basis, precision=lax.Precision.HIGH)
    on_cos = projected[:, :, :frames]
    on_sin = projected[:, :, frames:]
    out_real = on_cos[:, :branches] + on_sin[:, branches:]
    out_imag = on_cos[:, branches:] - on_sin[:, :branches]
    return (out_real * out_real + out_imag * out_imag) / frames


def solution(mesh):
    in_specs = (P("cell", "tm", None), P("cell", None), P(), P(("tm", "cell"), None, None, None))
    out_specs = P(("tm", "cell"), None, None)
    return jax.shard_map(local, mesh=mesh, in_specs=in_specs, out_specs=out_specs, check_vma=False)
```

```python
import math

import jax
import jax.numpy as jnp
from jax import lax
from jax.experimental import pallas as pl
from jax.experimental.pallas import tpu as pltpu
from jax.sharding import PartitionSpec as P
import numpy as np

L = 16


def quarter_tables():
    step = np.arange(4, dtype=np.float32) * np.float32(2.0 * math.pi / L)
    cos_k = np.cos(step).astype(jnp.bfloat16).astype(np.float32)
    sin_k = (-np.sin(step)).astype(jnp.bfloat16).astype(np.float32)
    return [float(v) for v in cos_k], [float(v) for v in sin_k]


def phase_block(c_ref, q_ref, block, group_width):
    cos_k, sin_k = quarter_tables()
    cells = c_ref[...].astype(jnp.float32).astype(jnp.bfloat16)
    points = q_ref[block].astype(jnp.float32).astype(jnp.bfloat16)
    dots = jnp.dot(cells, points, preferred_element_type=jnp.float32)
    m = dots.astype(jnp.int32) & (L - 1)
    bit0 = (m & 1) != 0
    bit1 = (m & 2) != 0
    bit2 = (m & 4) != 0
    bit3 = (m & 8) != 0
    real = jnp.where(bit1, jnp.where(bit0, cos_k[3], cos_k[2]), jnp.where(bit0, cos_k[1], cos_k[0]))
    imag = jnp.where(bit1, jnp.where(bit0, sin_k[3], sin_k[2]), jnp.where(bit0, sin_k[1], sin_k[0]))
    real, imag = jnp.where(bit2, imag, real), jnp.where(bit2, -real, imag)
    real, imag = jnp.where(bit3, -real, real), jnp.where(bit3, -imag, imag)
    column = lax.broadcasted_iota(jnp.int32, m.shape, 1) % group_width
    return jnp.where(column < group_width // 2, real, imag).astype(jnp.bfloat16)


def phase_sum_kernel(c_ref, q_ref, vt_ref, o_ref, phase_ref):
    per_step, _, group_width = o_ref.shape
    step = pl.program_id(0)
    steps = pl.num_programs(0)
    slot = step % 2

    @pl.when(step == 0)
    def _():
        phase_ref[0] = phase_block(c_ref, q_ref, 0, group_width)

    @pl.when(step + 1 < steps)
    def _():
        phase_ref[1 - slot] = phase_block(c_ref, q_ref, step + 1, group_width)

    sums = jnp.dot(vt_ref[...], phase_ref[slot], preferred_element_type=jnp.float32)
    for g in range(per_step):
        o_ref[g] = sums[:, g * group_width:(g + 1) * group_width].astype(o_ref.dtype)


def phase_sums(q_columns, cell_coords, velocity_t):
    groups, _, rows = q_columns.shape
    width, cells = velocity_t.shape
    pad = 8
    per_step = 2
    steps = groups // per_step
    block_width = per_step * 2 * rows
    c_in = jnp.pad(cell_coords, ((0, 0), (0, pad - 3)))
    q_in = jnp.concatenate([q_columns, q_columns], axis=2).transpose(1, 0, 2).reshape(3, steps, block_width)
    q_in = jnp.pad(q_in, ((0, pad - 3), (0, 0), (0, 0))).transpose(1, 0, 2)
    return pl.pallas_call(
        phase_sum_kernel,
        grid=(steps,),
        in_specs=[
            pl.BlockSpec((cells, pad), lambda i: (0, 0)),
            pl.BlockSpec((steps, pad, block_width), lambda i: (0, 0, 0)),
            pl.BlockSpec((width, cells), lambda i: (0, 0)),
        ],
        out_specs=pl.BlockSpec((per_step, width, 2 * rows), lambda i: (i, 0, 0)),
        out_shape=jax.ShapeDtypeStruct((groups, width, 2 * rows), jnp.bfloat16),
        scratch_shapes=[pltpu.VMEM((2, cells, block_width), jnp.bfloat16)],
        cost_estimate=pl.CostEstimate(
            flops=4 * groups * rows * cells * width,
            transcendentals=0,
            bytes_accessed=2 * cells * width + 4 * groups * rows * width,
        ),
    )(c_in, q_in, velocity_t)


def twiddles(frames):
    inner = 16
    outer = frames // inner
    w = jnp.arange(frames, dtype=jnp.int32)
    a = jnp.arange(outer, dtype=jnp.int32)
    b = jnp.arange(inner, dtype=jnp.int32)
    coarse = (a[:, None] * w[None, :] % outer).astype(jnp.float32) * (2.0 * math.pi / outer)
    fine = (b[:, None] * w[None, :] % frames).astype(jnp.float32) * (2.0 * math.pi / frames)
    cos_c, sin_c = jnp.cos(coarse)[:, None, :], jnp.sin(coarse)[:, None, :]
    cos_f, sin_f = jnp.cos(fine)[None, :, :], jnp.sin(fine)[None, :, :]
    cosines = (cos_c * cos_f - sin_c * sin_f).reshape(frames, frames)
    sines = (sin_c * cos_f + cos_c * sin_f).reshape(frames, frames)
    return cosines, sines


def local(velocity, cell_coords, q_coords, eigvecs):
    n_tm = lax.axis_size("tm")
    n_cell = lax.axis_size("cell")
    cell_dev, frames_dev, branches = velocity.shape
    q_total = q_coords.shape[0]
    q_local = q_total // (n_tm * n_cell)
    frames = frames_dev * n_tm
    q_columns = q_coords.reshape(n_tm, n_cell, q_local, 3).transpose(1, 3, 0, 2)
    q_columns = q_columns.reshape(n_cell, 3, n_tm * q_local)
    velocity_t = velocity.reshape(cell_dev, frames_dev * branches).T
    partial_term = phase_sums(q_columns, cell_coords, velocity_t)
    gathered = lax.all_to_all(partial_term, "cell", split_axis=0, concat_axis=0, tiled=True)
    summed = jnp.sum(gathered.astype(jnp.float32), axis=0).astype(jnp.bfloat16)
    blocks = summed.reshape(frames_dev, branches, 2, n_tm, q_local).transpose(3, 2, 4, 0, 1)
    collected = lax.all_to_all(blocks, "tm", split_axis=0, concat_axis=0, tiled=True)
    collected = collected.astype(jnp.float32)

    scale = 1.0 / math.sqrt(cell_dev * n_cell)
    e_real = eigvecs[:, 0] * scale
    e_imag = eigvecs[:, 1] * scale
    e_block = jnp.stack(
        [jnp.concatenate([e_real, -e_imag], axis=2), jnp.concatenate([e_imag, e_real], axis=2)],
        axis=1,
    )
    highest = lax.Precision.HIGHEST
    amplitude = jnp.einsum("arjtk,jrks->jats", collected, e_block, precision=highest).reshape(
        q_local, frames, 2 * branches
    )
    cosines, sines = twiddles(frames)
    basis = jnp.concatenate([cosines, sines], axis=1)
    projected = jnp.einsum("jts,tw->jsw", amplitude, basis, precision=lax.Precision.HIGH)
    on_cos = projected[:, :, :frames]
    on_sin = projected[:, :, frames:]
    out_real = on_cos[:, :branches] + on_sin[:, branches:]
    out_imag = on_cos[:, branches:] - on_sin[:, :branches]
    return (out_real * out_real + out_imag * out_imag) / frames


def solution(mesh):
    in_specs = (P("cell", "tm", None), P("cell", None), P(), P(("tm", "cell"), None, None, None))
    out_specs = P(("tm", "cell"), None, None)
    return jax.shard_map(local, mesh=mesh, in_specs=in_specs, out_specs=out_specs, check_vma=False)
```

```python
import math

import jax
import jax.numpy as jnp
from jax import lax
from jax.experimental import pallas as pl
from jax.experimental.pallas import tpu as pltpu
from jax.sharding import PartitionSpec as P
import numpy as np

L = 16


def quarter_tables():
    step = np.arange(4, dtype=np.float32) * np.float32(2.0 * math.pi / L)
    cos_k = np.cos(step).astype(jnp.bfloat16).astype(np.float32)
    sin_k = (-np.sin(step)).astype(jnp.bfloat16).astype(np.float32)
    return [float(v) for v in cos_k], [float(v) for v in sin_k]


def phase_block(c_ref, q_ref, block, group_width):
    cos_k, sin_k = quarter_tables()
    cells = c_ref[...].astype(jnp.float32).astype(jnp.bfloat16)
    points = q_ref[block].astype(jnp.float32).astype(jnp.bfloat16)
    dots = jnp.dot(cells, points, preferred_element_type=jnp.float32)
    m = dots.astype(jnp.int32) & (L - 1)
    bit0 = (m & 1) != 0
    bit1 = (m & 2) != 0
    bit2 = (m & 4) != 0
    bit3 = (m & 8) != 0
    real = jnp.where(bit1, jnp.where(bit0, cos_k[3], cos_k[2]), jnp.where(bit0, cos_k[1], cos_k[0]))
    imag = jnp.where(bit1, jnp.where(bit0, sin_k[3], sin_k[2]), jnp.where(bit0, sin_k[1], sin_k[0]))
    real, imag = jnp.where(bit2, imag, real), jnp.where(bit2, -real, imag)
    real, imag = jnp.where(bit3, -real, real), jnp.where(bit3, -imag, imag)
    column = lax.broadcasted_iota(jnp.int32, m.shape, 1) % group_width
    return jnp.where(column < group_width // 2, real, imag).astype(jnp.bfloat16)


def phase_sum_kernel(c_ref, q_ref, vt_ref, o_ref, phase_ref):
    per_step, _, group_width = o_ref.shape
    step = pl.program_id(0)
    steps = pl.num_programs(0)
    slot = step % 2

    @pl.when(step == 0)
    def _():
        phase_ref[0] = phase_block(c_ref, q_ref, 0, group_width)

    @pl.when(step + 1 < steps)
    def _():
        phase_ref[1 - slot] = phase_block(c_ref, q_ref, step + 1, group_width)

    sums = jnp.dot(vt_ref[...], phase_ref[slot], preferred_element_type=jnp.float32)
    for g in range(per_step):
        o_ref[g] = sums[:, g * group_width:(g + 1) * group_width].astype(o_ref.dtype)


def phase_sums(q_columns, cell_coords, velocity_t):
    groups, _, rows = q_columns.shape
    width, cells = velocity_t.shape
    pad = 8
    per_step = 2
    steps = groups // per_step
    block_width = per_step * 2 * rows
    c_in = jnp.pad(cell_coords, ((0, 0), (0, pad - 3)))
    q_in = jnp.concatenate([q_columns, q_columns], axis=2).transpose(1, 0, 2).reshape(3, steps, block_width)
    q_in = jnp.pad(q_in, ((0, pad - 3), (0, 0), (0, 0))).transpose(1, 0, 2)
    return pl.pallas_call(
        phase_sum_kernel,
        grid=(steps,),
        in_specs=[
            pl.BlockSpec((cells, pad), lambda i: (0, 0)),
            pl.BlockSpec((steps, pad, block_width), lambda i: (0, 0, 0)),
            pl.BlockSpec((width, cells), lambda i: (0, 0)),
        ],
        out_specs=pl.BlockSpec((per_step, width, 2 * rows), lambda i: (i, 0, 0)),
        out_shape=jax.ShapeDtypeStruct((groups, width, 2 * rows), jnp.bfloat16),
        scratch_shapes=[pltpu.VMEM((2, cells, block_width), jnp.bfloat16)],
        cost_estimate=pl.CostEstimate(
            flops=4 * groups * rows * cells * width,
            transcendentals=0,
            bytes_accessed=2 * cells * width + 4 * groups * rows * width,
        ),
    )(c_in, q_in, velocity_t)


def twiddles(frames):
    inner = 16
    outer = frames // inner
    w = jnp.arange(frames, dtype=jnp.int32)
    a = jnp.arange(outer, dtype=jnp.int32)
    b = jnp.arange(inner, dtype=jnp.int32)
    coarse = (a[:, None] * w[None, :] % outer).astype(jnp.float32) * (2.0 * math.pi / outer)
    fine = (b[:, None] * w[None, :] % frames).astype(jnp.float32) * (2.0 * math.pi / frames)
    cos_c, sin_c = jnp.cos(coarse)[:, None, :], jnp.sin(coarse)[:, None, :]
    cos_f, sin_f = jnp.cos(fine)[None, :, :], jnp.sin(fine)[None, :, :]
    cosines = (cos_c * cos_f - sin_c * sin_f).reshape(frames, frames)
    sines = (sin_c * cos_f + cos_c * sin_f).reshape(frames, frames)
    return cosines, sines


def local(velocity, cell_coords, q_coords, eigvecs):
    n_tm = lax.axis_size("tm")
    n_cell = lax.axis_size("cell")
    cell_dev, frames_dev, branches = velocity.shape
    q_total = q_coords.shape[0]
    q_local = q_total // (n_tm * n_cell)
    frames = frames_dev * n_tm
    q_columns = q_coords.reshape(n_tm, n_cell, q_local, 3).transpose(1, 3, 0, 2)
    q_columns = q_columns.reshape(n_cell, 3, n_tm * q_local)
    velocity_t = velocity.reshape(cell_dev, frames_dev * branches).T
    partial_term = phase_sums(q_columns, cell_coords, velocity_t)
    gathered = lax.all_to_all(partial_term, "cell", split_axis=0, concat_axis=0, tiled=True)
    summed = jnp.sum(gathered.astype(jnp.float32), axis=0).astype(jnp.bfloat16)
    blocks = summed.reshape(frames_dev, branches, 2, n_tm, q_local).transpose(3, 2, 4, 0, 1)
    collected = lax.all_to_all(blocks, "tm", split_axis=0, concat_axis=0, tiled=True)
    collected = collected.astype(jnp.float32)

    scale = 1.0 / math.sqrt(cell_dev * n_cell)
    e_real = eigvecs[:, 0] * scale
    e_imag = eigvecs[:, 1] * scale
    e_block = jnp.stack(
        [jnp.concatenate([e_real, -e_imag], axis=2), jnp.concatenate([e_imag, e_real], axis=2)],
        axis=1,
    )
    highest = lax.Precision.HIGHEST
    amplitude = jnp.einsum("arjtk,jrks->jats", collected, e_block, precision=highest).reshape(
        q_local, frames, 2 * branches
    )
    cosines, sines = twiddles(frames)
    basis = jnp.concatenate([cosines, sines], axis=1)
    projected = jnp.einsum(
        "jts,tw->jsw", amplitude.astype(jnp.bfloat16), basis.astype(jnp.bfloat16),
        preferred_element_type=jnp.float32,
    )
    on_cos = projected[:, :, :frames]
    on_sin = projected[:, :, frames:]
    out_real = on_cos[:, :branches] + on_sin[:, branches:]
    out_imag = on_cos[:, branches:] - on_sin[:, :branches]
    return (out_real * out_real + out_imag * out_imag) / frames


def solution(mesh):
    in_specs = (P("cell", "tm", None), P("cell", None), P(), P(("tm", "cell"), None, None, None))
    out_specs = P(("tm", "cell"), None, None)
    return jax.shard_map(local, mesh=mesh, in_specs=in_specs, out_specs=out_specs, check_vma=False)
```

```python
import math

import jax
import jax.numpy as jnp
from jax import lax
from jax.experimental import pallas as pl
from jax.experimental.pallas import tpu as pltpu
from jax.sharding import PartitionSpec as P
import numpy as np

L = 16


def quarter_tables():
    step = np.arange(4, dtype=np.float32) * np.float32(2.0 * math.pi / L)
    cos_k = np.cos(step).astype(jnp.bfloat16).astype(np.float32)
    sin_k = (-np.sin(step)).astype(jnp.bfloat16).astype(np.float32)
    return [float(v) for v in cos_k], [float(v) for v in sin_k]


def phase_block(c_ref, q_ref, block, group_width):
    cos_k, sin_k = quarter_tables()
    cells = c_ref[...].astype(jnp.float32).astype(jnp.bfloat16)
    points = q_ref[block].astype(jnp.float32).astype(jnp.bfloat16)
    dots = jnp.dot(cells, points, preferred_element_type=jnp.float32)
    m = dots.astype(jnp.int32) & (L - 1)
    bit0 = (m & 1) != 0
    bit1 = (m & 2) != 0
    bit2 = (m & 4) != 0
    bit3 = (m & 8) != 0
    real = jnp.where(bit1, jnp.where(bit0, cos_k[3], cos_k[2]), jnp.where(bit0, cos_k[1], cos_k[0]))
    imag = jnp.where(bit1, jnp.where(bit0, sin_k[3], sin_k[2]), jnp.where(bit0, sin_k[1], sin_k[0]))
    real, imag = jnp.where(bit2, imag, real), jnp.where(bit2, -real, imag)
    real, imag = jnp.where(bit3, -real, real), jnp.where(bit3, -imag, imag)
    column = lax.broadcasted_iota(jnp.int32, m.shape, 1) % group_width
    return jnp.where(column < group_width // 2, real, imag).astype(jnp.bfloat16)


def phase_sum_kernel(c_ref, q_ref, vt_ref, o_ref, phase_ref):
    per_step, _, group_width = o_ref.shape
    step = pl.program_id(0)
    steps = pl.num_programs(0)
    slot = step % 2

    @pl.when(step == 0)
    def _():
        phase_ref[0] = phase_block(c_ref, q_ref, 0, group_width)

    @pl.when(step + 1 < steps)
    def _():
        phase_ref[1 - slot] = phase_block(c_ref, q_ref, step + 1, group_width)

    sums = jnp.dot(vt_ref[...], phase_ref[slot], preferred_element_type=jnp.float32)
    for g in range(per_step):
        o_ref[g] = sums[:, g * group_width:(g + 1) * group_width].astype(o_ref.dtype)


def phase_sums(q_columns, cell_coords, velocity_t):
    groups, _, rows = q_columns.shape
    width, cells = velocity_t.shape
    pad = 3
    per_step = 2
    steps = groups // per_step
    block_width = per_step * 2 * rows
    c_in = cell_coords
    q_in = jnp.concatenate([q_columns, q_columns], axis=2).transpose(1, 0, 2).reshape(3, steps, block_width)
    q_in = q_in.transpose(1, 0, 2)
    return pl.pallas_call(
        phase_sum_kernel,
        grid=(steps,),
        in_specs=[
            pl.BlockSpec((cells, pad), lambda i: (0, 0)),
            pl.BlockSpec((steps, pad, block_width), lambda i: (0, 0, 0)),
            pl.BlockSpec((width, cells), lambda i: (0, 0)),
        ],
        out_specs=pl.BlockSpec((per_step, width, 2 * rows), lambda i: (i, 0, 0)),
        out_shape=jax.ShapeDtypeStruct((groups, width, 2 * rows), jnp.bfloat16),
        scratch_shapes=[pltpu.VMEM((2, cells, block_width), jnp.bfloat16)],
        cost_estimate=pl.CostEstimate(
            flops=4 * groups * rows * cells * width,
            transcendentals=0,
            bytes_accessed=2 * cells * width + 4 * groups * rows * width,
        ),
    )(c_in, q_in, velocity_t)


def twiddles(frames):
    inner = 16
    outer = frames // inner
    w = jnp.arange(frames, dtype=jnp.int32)
    a = jnp.arange(outer, dtype=jnp.int32)
    b = jnp.arange(inner, dtype=jnp.int32)
    coarse = (a[:, None] * w[None, :] % outer).astype(jnp.float32) * (2.0 * math.pi / outer)
    fine = (b[:, None] * w[None, :] % frames).astype(jnp.float32) * (2.0 * math.pi / frames)
    cos_c, sin_c = jnp.cos(coarse)[:, None, :], jnp.sin(coarse)[:, None, :]
    cos_f, sin_f = jnp.cos(fine)[None, :, :], jnp.sin(fine)[None, :, :]
    cosines = (cos_c * cos_f - sin_c * sin_f).reshape(frames, frames)
    sines = (sin_c * cos_f + cos_c * sin_f).reshape(frames, frames)
    return cosines, sines


def local(velocity, cell_coords, q_coords, eigvecs):
    n_tm = lax.axis_size("tm")
    n_cell = lax.axis_size("cell")
    cell_dev, frames_dev, branches = velocity.shape
    q_total = q_coords.shape[0]
    q_local = q_total // (n_tm * n_cell)
    frames = frames_dev * n_tm
    q_columns = q_coords.reshape(n_tm, n_cell, q_local, 3).transpose(1, 3, 0, 2)
    q_columns = q_columns.reshape(n_cell, 3, n_tm * q_local)
    velocity_t = velocity.reshape(cell_dev, frames_dev * branches).T
    partial_term = phase_sums(q_columns, cell_coords, velocity_t)
    gathered = lax.all_to_all(partial_term, "cell", split_axis=0, concat_axis=0, tiled=True)
    summed = jnp.sum(gathered.astype(jnp.float32), axis=0).astype(jnp.bfloat16)
    blocks = summed.reshape(frames_dev, branches, 2, n_tm, q_local).transpose(3, 2, 4, 0, 1)
    collected = lax.all_to_all(blocks, "tm", split_axis=0, concat_axis=0, tiled=True)

    scale = 1.0 / math.sqrt(cell_dev * n_cell)
    e_real = eigvecs[:, 0] * scale
    e_imag = eigvecs[:, 1] * scale
    e_block = jnp.stack(
        [jnp.concatenate([e_real, -e_imag], axis=2), jnp.concatenate([e_imag, e_real], axis=2)],
        axis=1,
    )
    amplitude = jnp.einsum(
        "arjtk,jrks->jats", collected, e_block.astype(jnp.bfloat16), preferred_element_type=jnp.float32
    ).reshape(
        q_local, frames, 2 * branches
    )
    cosines, sines = twiddles(frames)
    basis = jnp.concatenate([cosines, sines], axis=1)
    projected = jnp.einsum(
        "jts,tw->jsw", amplitude.astype(jnp.bfloat16), basis.astype(jnp.bfloat16),
        preferred_element_type=jnp.float32,
    )
    on_cos = projected[:, :, :frames]
    on_sin = projected[:, :, frames:]
    out_real = on_cos[:, :branches] + on_sin[:, branches:]
    out_imag = on_cos[:, branches:] - on_sin[:, :branches]
    return (out_real * out_real + out_imag * out_imag) / frames


def solution(mesh):
    in_specs = (P("cell", "tm", None), P("cell", None), P(), P(("tm", "cell"), None, None, None))
    out_specs = P(("tm", "cell"), None, None)
    return jax.shard_map(local, mesh=mesh, in_specs=in_specs, out_specs=out_specs, check_vma=False)
```

```python
import math

import jax
import jax.numpy as jnp
from jax import lax
from jax.experimental import pallas as pl
from jax.experimental.pallas import tpu as pltpu
from jax.sharding import PartitionSpec as P
import numpy as np

L = 16


def quarter_tables():
    step = np.arange(4, dtype=np.float32) * np.float32(2.0 * math.pi / L)
    cos_k = np.cos(step).astype(jnp.bfloat16).astype(np.float32)
    sin_k = (-np.sin(step)).astype(jnp.bfloat16).astype(np.float32)
    return [float(v) for v in cos_k], [float(v) for v in sin_k]


def phase_block(c_ref, q_ref, block, group_width):
    cos_k, sin_k = quarter_tables()
    cells = c_ref[...].astype(jnp.float32).astype(jnp.bfloat16)
    points = q_ref[block].astype(jnp.float32).astype(jnp.bfloat16)
    dots = jnp.dot(cells, points, preferred_element_type=jnp.float32)
    m = dots.astype(jnp.int32) & (L - 1)
    bit0 = (m & 1) != 0
    bit1 = (m & 2) != 0
    bit2 = (m & 4) != 0
    bit3 = (m & 8) != 0
    real = jnp.where(bit1, jnp.where(bit0, cos_k[3], cos_k[2]), jnp.where(bit0, cos_k[1], cos_k[0]))
    imag = jnp.where(bit1, jnp.where(bit0, sin_k[3], sin_k[2]), jnp.where(bit0, sin_k[1], sin_k[0]))
    real, imag = jnp.where(bit2, imag, real), jnp.where(bit2, -real, imag)
    real, imag = jnp.where(bit3, -real, real), jnp.where(bit3, -imag, imag)
    column = lax.broadcasted_iota(jnp.int32, m.shape, 1) % group_width
    return jnp.where(column < group_width // 2, real, imag).astype(jnp.bfloat16)


def phase_sum_kernel(c_ref, q_ref, vt_ref, o_ref, phase_ref):
    per_step, _, group_width = o_ref.shape
    step = pl.program_id(0)
    steps = pl.num_programs(0)
    slot = step % 2

    @pl.when(step == 0)
    def _():
        phase_ref[0] = phase_block(c_ref, q_ref, 0, group_width)

    @pl.when(step + 1 < steps)
    def _():
        phase_ref[1 - slot] = phase_block(c_ref, q_ref, step + 1, group_width)

    sums = jnp.dot(vt_ref[...], phase_ref[slot], preferred_element_type=jnp.float32)
    for g in range(per_step):
        o_ref[g] = sums[:, g * group_width:(g + 1) * group_width].astype(o_ref.dtype)


def phase_sums(q_columns, cell_coords, velocity_t):
    groups, _, rows = q_columns.shape
    width, cells = velocity_t.shape
    pad = 8
    per_step = 4
    steps = groups // per_step
    block_width = per_step * 2 * rows
    c_in = jnp.pad(cell_coords, ((0, 0), (0, pad - 3)))
    q_in = jnp.concatenate([q_columns, q_columns], axis=2).transpose(1, 0, 2).reshape(3, steps, block_width)
    q_in = jnp.pad(q_in, ((0, pad - 3), (0, 0), (0, 0))).transpose(1, 0, 2)
    return pl.pallas_call(
        phase_sum_kernel,
        grid=(steps,),
        in_specs=[
            pl.BlockSpec((cells, pad), lambda i: (0, 0)),
            pl.BlockSpec((steps, pad, block_width), lambda i: (0, 0, 0)),
            pl.BlockSpec((width, cells), lambda i: (0, 0)),
        ],
        out_specs=pl.BlockSpec((per_step, width, 2 * rows), lambda i: (i, 0, 0)),
        out_shape=jax.ShapeDtypeStruct((groups, width, 2 * rows), jnp.bfloat16),
        scratch_shapes=[pltpu.VMEM((2, cells, block_width), jnp.bfloat16)],
        cost_estimate=pl.CostEstimate(
            flops=4 * groups * rows * cells * width,
            transcendentals=0,
            bytes_accessed=2 * cells * width + 4 * groups * rows * width,
        ),
    )(c_in, q_in, velocity_t)


def twiddles(frames):
    inner = 16
    outer = frames // inner
    w = jnp.arange(frames, dtype=jnp.int32)
    a = jnp.arange(outer, dtype=jnp.int32)
    b = jnp.arange(inner, dtype=jnp.int32)
    coarse = (a[:, None] * w[None, :] % outer).astype(jnp.float32) * (2.0 * math.pi / outer)
    fine = (b[:, None] * w[None, :] % frames).astype(jnp.float32) * (2.0 * math.pi / frames)
    cos_c, sin_c = jnp.cos(coarse)[:, None, :], jnp.sin(coarse)[:, None, :]
    cos_f, sin_f = jnp.cos(fine)[None, :, :], jnp.sin(fine)[None, :, :]
    cosines = (cos_c * cos_f - sin_c * sin_f).reshape(frames, frames)
    sines = (sin_c * cos_f + cos_c * sin_f).reshape(frames, frames)
    return cosines, sines


def local(velocity, cell_coords, q_coords, eigvecs):
    n_tm = lax.axis_size("tm")
    n_cell = lax.axis_size("cell")
    cell_dev, frames_dev, branches = velocity.shape
    q_total = q_coords.shape[0]
    q_local = q_total // (n_tm * n_cell)
    frames = frames_dev * n_tm
    q_columns = q_coords.reshape(n_tm, n_cell, q_local, 3).transpose(1, 3, 0, 2)
    q_columns = q_columns.reshape(n_cell, 3, n_tm * q_local)
    velocity_t = velocity.reshape(cell_dev, frames_dev * branches).T
    partial_term = phase_sums(q_columns, cell_coords, velocity_t)
    gathered = lax.all_to_all(partial_term, "cell", split_axis=0, concat_axis=0, tiled=True)
    summed = jnp.sum(gathered.astype(jnp.float32), axis=0).astype(jnp.bfloat16)
    blocks = summed.reshape(frames_dev, branches, 2, n_tm, q_local).transpose(3, 2, 4, 0, 1)
    collected = lax.all_to_all(blocks, "tm", split_axis=0, concat_axis=0, tiled=True)
    collected = collected.astype(jnp.float32)

    scale = 1.0 / math.sqrt(cell_dev * n_cell)
    e_real = eigvecs[:, 0] * scale
    e_imag = eigvecs[:, 1] * scale
    e_block = jnp.stack(
        [jnp.concatenate([e_real, -e_imag], axis=2), jnp.concatenate([e_imag, e_real], axis=2)],
        axis=1,
    )
    highest = lax.Precision.HIGHEST
    amplitude = jnp.einsum("arjtk,jrks->jats", collected, e_block, precision=highest).reshape(
        q_local, frames, 2 * branches
    )
    cosines, sines = twiddles(frames)
    basis = jnp.concatenate([cosines, sines], axis=1)
    projected = jnp.einsum(
        "jts,tw->jsw", amplitude.astype(jnp.bfloat16), basis.astype(jnp.bfloat16),
        preferred_element_type=jnp.float32,
    )
    on_cos = projected[:, :, :frames]
    on_sin = projected[:, :, frames:]
    out_real = on_cos[:, :branches] + on_sin[:, branches:]
    out_imag = on_cos[:, branches:] - on_sin[:, :branches]
    return (out_real * out_real + out_imag * out_imag) / frames


def solution(mesh):
    in_specs = (P("cell", "tm", None), P("cell", None), P(), P(("tm", "cell"), None, None, None))
    out_specs = P(("tm", "cell"), None, None)
    return jax.shard_map(local, mesh=mesh, in_specs=in_specs, out_specs=out_specs, check_vma=False)
```

```python
import math

import jax
import jax.numpy as jnp
from jax import lax
from jax.experimental import pallas as pl
from jax.experimental.pallas import tpu as pltpu
from jax.sharding import PartitionSpec as P
import numpy as np

L = 16


def quarter_tables():
    step = np.arange(4, dtype=np.float32) * np.float32(2.0 * math.pi / L)
    cos_k = np.cos(step).astype(jnp.bfloat16).astype(np.float32)
    sin_k = (-np.sin(step)).astype(jnp.bfloat16).astype(np.float32)
    return [float(v) for v in cos_k], [float(v) for v in sin_k]


def phase_block(c_ref, q_ref, block, group_width):
    cos_k, sin_k = quarter_tables()
    cells = c_ref[...].astype(jnp.float32).astype(jnp.bfloat16)
    points = q_ref[block].astype(jnp.float32).astype(jnp.bfloat16)
    dots = jnp.dot(cells, points, preferred_element_type=jnp.float32)
    m = dots.astype(jnp.int32) & (L - 1)
    bit0 = (m & 1) != 0
    bit1 = (m & 2) != 0
    bit2 = (m & 4) != 0
    bit3 = (m & 8) != 0
    real = jnp.where(bit1, jnp.where(bit0, cos_k[3], cos_k[2]), jnp.where(bit0, cos_k[1], cos_k[0]))
    imag = jnp.where(bit1, jnp.where(bit0, sin_k[3], sin_k[2]), jnp.where(bit0, sin_k[1], sin_k[0]))
    real, imag = jnp.where(bit2, imag, real), jnp.where(bit2, -real, imag)
    real, imag = jnp.where(bit3, -real, real), jnp.where(bit3, -imag, imag)
    column = lax.broadcasted_iota(jnp.int32, m.shape, 1) % group_width
    return jnp.where(column < group_width // 2, real, imag).astype(jnp.bfloat16)


def phase_sum_kernel(c_ref, q_ref, vt_ref, o_ref, phase_ref):
    per_step, _, group_width = o_ref.shape
    step = pl.program_id(0)
    steps = pl.num_programs(0)
    slot = step % 2

    @pl.when(step == 0)
    def _():
        phase_ref[0] = phase_block(c_ref, q_ref, 0, group_width)

    @pl.when(step + 1 < steps)
    def _():
        phase_ref[1 - slot] = phase_block(c_ref, q_ref, step + 1, group_width)

    sums = jnp.dot(vt_ref[...], phase_ref[slot], preferred_element_type=jnp.float32)
    for g in range(per_step):
        o_ref[g] = sums[:, g * group_width:(g + 1) * group_width].astype(o_ref.dtype)


def phase_sums(q_columns, cell_coords, velocity_t):
    groups, _, rows = q_columns.shape
    width, cells = velocity_t.shape
    pad = 8
    per_step = 4
    steps = groups // per_step
    block_width = per_step * 2 * rows
    c_in = jnp.pad(cell_coords, ((0, 0), (0, pad - 3)))
    q_in = jnp.concatenate([q_columns, q_columns], axis=2).transpose(1, 0, 2).reshape(3, steps, block_width)
    q_in = jnp.pad(q_in, ((0, pad - 3), (0, 0), (0, 0))).transpose(1, 0, 2)
    return pl.pallas_call(
        phase_sum_kernel,
        grid=(steps,),
        in_specs=[
            pl.BlockSpec((cells, pad), lambda i: (0, 0)),
            pl.BlockSpec((steps, pad, block_width), lambda i: (0, 0, 0)),
            pl.BlockSpec((width, cells), lambda i: (0, 0)),
        ],
        out_specs=pl.BlockSpec((per_step, width, 2 * rows), lambda i: (i, 0, 0)),
        out_shape=jax.ShapeDtypeStruct((groups, width, 2 * rows), jnp.bfloat16),
        scratch_shapes=[pltpu.VMEM((2, cells, block_width), jnp.bfloat16)],
        cost_estimate=pl.CostEstimate(
            flops=4 * groups * rows * cells * width,
            transcendentals=0,
            bytes_accessed=2 * cells * width + 4 * groups * rows * width,
        ),
    )(c_in, q_in, velocity_t)


def twiddles(frames):
    inner = 16
    outer = frames // inner
    w = jnp.arange(frames, dtype=jnp.int32)
    a = jnp.arange(outer, dtype=jnp.int32)
    b = jnp.arange(inner, dtype=jnp.int32)
    coarse = (a[:, None] * w[None, :] % outer).astype(jnp.float32) * (2.0 * math.pi / outer)
    fine = (b[:, None] * w[None, :] % frames).astype(jnp.float32) * (2.0 * math.pi / frames)
    cos_c, sin_c = jnp.cos(coarse)[:, None, :], jnp.sin(coarse)[:, None, :]
    cos_f, sin_f = jnp.cos(fine)[None, :, :], jnp.sin(fine)[None, :, :]
    cosines = (cos_c * cos_f - sin_c * sin_f).reshape(frames, frames)
    sines = (sin_c * cos_f + cos_c * sin_f).reshape(frames, frames)
    return cosines, sines


def local(velocity, cell_coords, q_coords, eigvecs):
    n_tm = lax.axis_size("tm")
    n_cell = lax.axis_size("cell")
    cell_dev, frames_dev, branches = velocity.shape
    q_total = q_coords.shape[0]
    q_local = q_total // (n_tm * n_cell)
    frames = frames_dev * n_tm
    q_columns = q_coords.reshape(n_tm, n_cell, q_local, 3).transpose(1, 3, 0, 2)
    q_columns = q_columns.reshape(n_cell, 3, n_tm * q_local)
    velocity_t = velocity.reshape(cell_dev, frames_dev * branches).T
    partial_term = phase_sums(q_columns, cell_coords, velocity_t)
    gathered = lax.all_to_all(partial_term, "cell", split_axis=0, concat_axis=0, tiled=True)
    summed = jnp.sum(gathered.astype(jnp.float32), axis=0).astype(jnp.bfloat16)
    blocks = summed.reshape(frames_dev, branches, 2, n_tm, q_local).transpose(3, 2, 4, 0, 1)
    collected = lax.all_to_all(blocks, "tm", split_axis=0, concat_axis=0, tiled=True)

    scale = 1.0 / math.sqrt(cell_dev * n_cell)
    e_real = eigvecs[:, 0] * scale
    e_imag = eigvecs[:, 1] * scale
    e_block = jnp.stack(
        [jnp.concatenate([e_real, -e_imag], axis=2), jnp.concatenate([e_imag, e_real], axis=2)],
        axis=1,
    )
    amplitude = jnp.einsum(
        "arjtk,jrks->jats", collected, e_block.astype(jnp.bfloat16), preferred_element_type=jnp.float32
    ).reshape(
        q_local, frames, 2 * branches
    )
    cosines, sines = twiddles(frames)
    basis = jnp.concatenate([cosines, sines], axis=1)
    projected = jnp.einsum(
        "jts,tw->jsw", amplitude.astype(jnp.bfloat16), basis.astype(jnp.bfloat16),
        preferred_element_type=jnp.float32,
    )
    on_cos = projected[:, :, :frames]
    on_sin = projected[:, :, frames:]
    out_real = on_cos[:, :branches] + on_sin[:, branches:]
    out_imag = on_cos[:, branches:] - on_sin[:, :branches]
    return (out_real * out_real + out_imag * out_imag) / frames


def solution(mesh):
    in_specs = (P("cell", "tm", None), P("cell", None), P(), P(("tm", "cell"), None, None, None))
    out_specs = P(("tm", "cell"), None, None)
    return jax.shard_map(local, mesh=mesh, in_specs=in_specs, out_specs=out_specs, check_vma=False)
```
